32 devices in a mesh: blk: 16 (over z, y, core), rel: 2 (over x).
Axes of the slice: x: 2, y: 2, z: 4, core: 2. Of those that a mesh axis runs over, the one named last changes fastest.
Arguments:
- words: bfloat16 [4096, 800], P('blk'), may hold values from -1.5 to 1.5
- contexts: bfloat16 [4096, 800], P('blk'), may hold values from -1.5 to 1.5
- relations: bfloat16 [1024, 800], P(('blk', 'rel')), may hold values from -6 to 6
- word_index: int32 [8192], P(('blk', 'rel')), may hold values from 0 to 255
- context_index: int32 [8192], P(('blk', 'rel')), may hold values from 0 to 255
- rel_slot: int32 [8192], P(('blk', 'rel')), may hold values from 0 to 63, as said below
- neg_index: int32 [32, 1024], P(('blk', 'rel')), may hold values from 0 to 255
- requests: int32 [16, 2, 16, 2, 2], P('blk', 'rel'), may hold values from 0 to 31, as said below
- counts: int32 [16, 2, 16, 2], P('blk', 'rel'), may hold values from 0 to 2, as said below
Outputs:
- word_grad: bfloat16 [4096, 800], P('blk')
- context_grad: bfloat16 [4096, 800], P('blk')
- relation_grad: float32 [1024, 800], P(('blk', 'rel'))
The draws below stay inside these ranges and needn't reach their ends.
Inputs may be any that keep to these rules, and one draw needn't show every extreme that they name: counts[b, r, b2, r2] is how many entries of the list of device (b, r) to owner (b2, r2) are live; each device's list to itself is full, and so are all lists to one owner. requests[b, r, b2, r2, k] is a row among the 32 relation rows of owner (b2, r2); the live entries of one list are distinct and come first, the others are 0. rel_slot of a triple of device (b, r) is a live slot s = (b2 * 2 + r2) * 2 + k of that device, with k < counts[b, r, b2, r2].
All inputs are finite; a program needn't handle non-finite values.
Results may differ from the reference program's by a relative error of at most 0.013.
Values may be sent and summed in bfloat16 or wider, within the bound.
No kernel may reach another device: no remote copies, remote signals or barrier semaphores. Data moves between devices by JAX's collectives and lax.ppermute only.
A program may use at most 64 MiB of HBM per device.

```python
import jax
import jax.numpy as jnp
from jax import lax

RANK = 400
PART = 256
BLOCK = 256
NEG = 1024
BLOCKS = 1
SLOTS = 2
REL_DEV = 32
ENT_PARTS = 16
REL_SPLIT = 2
OWNERS = 32
TRIPS = 256
NWORD = 4096
NREL = 1024
NTRIP = 8192
NBLOCKS = 32


def bucket_plan(key):
    owner_count = ENT_PARTS * REL_SPLIT
    base_key = jax.random.fold_in(key, 7)
    key_hot, key_base, key_full, key_start, key_step = jax.random.split(base_key, 5)
    hotness = jax.random.randint(key_hot, (owner_count,), 0, 3)
    base_counts = jax.random.randint(key_base, (owner_count, owner_count), 0, SLOTS + 1)
    live_counts = jnp.minimum(base_counts + hotness[None, :], SLOTS)
    full_owner = jax.random.randint(key_full, (), 0, owner_count)
    owner_ids = jnp.arange(owner_count)
    forced = (owner_ids[None, :] == owner_ids[:, None]) | (owner_ids[None, :] == full_owner)
    live_counts = jnp.where(forced, SLOTS, live_counts).astype(jnp.int32)
    starts = jax.random.randint(key_start, (owner_count, owner_count, 1), 0, REL_DEV)
    strides = 2 * jax.random.randint(key_step, (owner_count, owner_count, 1), 0, REL_DEV // 2) + 1
    positions = jnp.arange(SLOTS)[None, None, :]
    wanted_rows = (starts + strides * positions) % REL_DEV
    wanted_rows = jnp.where(positions < live_counts[:, :, None], wanted_rows, 0).astype(jnp.int32)
    return (live_counts, wanted_rows)


def draw_requests(key, part):
    live_counts, wanted_rows = bucket_plan(key)
    return wanted_rows.reshape(ENT_PARTS, REL_SPLIT, ENT_PARTS, REL_SPLIT, SLOTS)


def draw_counts(key, part):
    live_counts, wanted_rows = bucket_plan(key)
    return live_counts.reshape(ENT_PARTS, REL_SPLIT, ENT_PARTS, REL_SPLIT)


def draw_rel_slot(key, part):
    owner_count = ENT_PARTS * REL_SPLIT
    live_counts, wanted_rows = bucket_plan(key)
    live_mask = (jnp.arange(SLOTS)[None, None, :] < live_counts[:, :, None]).reshape(owner_count, owner_count * SLOTS).astype(jnp.int32)
    order_ids = jnp.argsort(1 - live_mask, axis=1, stable=True).astype(jnp.int32)
    live_total = jnp.sum(live_mask, axis=1)
    picks = jax.random.randint(jax.random.fold_in(key, 11), (owner_count, TRIPS), 0, live_total[:, None])
    chosen = jnp.take_along_axis(order_ids, picks, axis=1)
    return chosen.reshape(-1).astype(jnp.int32)


def with_ends(entries, key, smallest, high):
    shape = entries.shape
    place = [jax.random.randint(jax.random.fold_in(key, axis), (), 0, shape[axis]) for axis in range(len(shape))]
    entries = entries.at[tuple(place)].set(smallest)
    longest = shape.index(max(shape))
    place[longest] = (place[longest] + 1) % shape[longest]
    return entries.at[tuple(place)].set(high)


def block_levels(rng, extent, cuts, low, top_value):
    def one(position, shards_of):
        draws = jax.random.uniform(jax.random.fold_in(jax.random.fold_in(rng, 6), position), (shards_of,), jnp.float32, low / len(cuts), top_value / len(cuts))
        return jnp.repeat(jnp.exp(draws), extent[position] // shards_of).reshape((-1,) + (1,) * (len(extent) - position - 1))

    loudness = one(*cuts[0])
    for cut in cuts[1:]:
        loudness = loudness * one(*cut)
    return loudness


def bell_draw(own_key, extent, width, bound, cuts=(), held_as=jnp.bfloat16):
    loudness = block_levels(own_key, extent, cuts, -0.22, 0.18) if cuts else 1.0
    result = jax.random.normal(own_key, extent, jnp.float32) * width * loudness
    return jnp.minimum(jnp.maximum(result, -bound), bound).astype(held_as)


def setup_inputs(seed: int = 0) -> dict:
    streams_of = jax.random.split(jax.random.key(seed), 10)
    return {
        "words": bell_draw(streams_of[0], (NWORD, 2 * RANK), 0.25, 1.5, ((0, 16),)),
        "contexts": bell_draw(streams_of[1], (NWORD, 2 * RANK), 0.25, 1.5, ((0, 16),)),
        "relations": bell_draw(streams_of[2], (NREL, 2 * RANK), 1.0, 6.0, ((0, 32),)),
        "word_index": with_ends(jax.random.randint(streams_of[3], (NTRIP,), 0, PART), jax.random.fold_in(streams_of[3], 1), 0, PART - 1).astype(jnp.int32),
        "context_index": with_ends(jax.random.randint(streams_of[4], (NTRIP,), 0, PART), jax.random.fold_in(streams_of[4], 1), 0, PART - 1).astype(jnp.int32),
        "rel_slot": draw_rel_slot(jax.random.fold_in(streams_of[9], 71), 0),
        "neg_index": with_ends(jax.random.randint(streams_of[6], (NBLOCKS, NEG), 0, PART), jax.random.fold_in(streams_of[6], 1), 0, PART - 1).astype(jnp.int32),
        "requests": draw_requests(jax.random.fold_in(streams_of[9], 71), 0),
        "counts": draw_counts(jax.random.fold_in(streams_of[9], 71), 0),
    }


def complex_product(left_vec, right_vec):
    left_re, left_im = left_vec[:, :RANK], left_vec[:, RANK:]
    right_re, right_im = right_vec[:, :RANK], right_vec[:, RANK:]
    return jnp.concatenate([left_re * right_re - left_im * right_im, left_re * right_im + left_im * right_re], axis=1)


def conj_product(grad_vec, other_vec):
    grad_re, grad_im = grad_vec[:, :RANK], grad_vec[:, RANK:]
    other_re, other_im = other_vec[:, :RANK], other_vec[:, RANK:]
    return jnp.concatenate([grad_re * other_re + grad_im * other_im, grad_im * other_re - grad_re * other_im], axis=1)


def one_device(relations, word_rows, held_rows, word_ids, ctx_ids, slot_ids, neg_ids, wanted, live_count):
    row_width = 2 * RANK
    slot_total = OWNERS * SLOTS
    live_mask = (jnp.arange(SLOTS)[None, :] < live_count[:, None]).reshape(-1).astype(jnp.float32)
    relation_ids = ((jnp.arange(slot_total) // SLOTS) * REL_DEV + wanted).astype(jnp.int32)
    slot_table = relations[relation_ids]
    word_used = word_rows[word_ids]
    ctx_used = held_rows[ctx_ids]
    rel_used = slot_table[slot_ids]
    query = complex_product(word_used.astype(jnp.float32), rel_used.astype(jnp.float32)).astype(jnp.bfloat16)
    positive = jnp.sum(query.astype(jnp.float32) * ctx_used.astype(jnp.float32), axis=1)
    pos_grad = -jax.nn.sigmoid(-positive)
    ctx_start = jnp.zeros((PART, row_width), jnp.float32).at[ctx_ids].add(pos_grad[:, None] * query.astype(jnp.float32))
    neg_scale = NEG ** -0.5

    def block_step(ctx_total, inputs_one):
        query_block, ctx_block, neg_block, pos_block = inputs_one
        neg_rows = held_rows[neg_block]
        scores = jnp.dot(query_block, neg_rows.T, preferred_element_type=jnp.float32)
        neg_grad = (jax.nn.sigmoid(scores) * neg_scale).astype(jnp.bfloat16)
        query_grad = pos_block[:, None] * ctx_block.astype(jnp.float32) + jnp.dot(neg_grad, neg_rows, preferred_element_type=jnp.float32)
        back_rows = jnp.dot(neg_grad.T, query_block, preferred_element_type=jnp.float32)
        return ctx_total.at[neg_block].add(back_rows), query_grad

    ctx_part, query_grads = lax.scan(block_step, ctx_start, (query.reshape(BLOCKS, BLOCK, row_width), ctx_used.reshape(BLOCKS, BLOCK, row_width), neg_ids, pos_grad.reshape(BLOCKS, BLOCK)))
    query_grads = query_grads.reshape(TRIPS, row_width)
    word_part = jnp.zeros((PART, row_width), jnp.float32).at[word_ids].add(conj_product(query_grads, rel_used.astype(jnp.float32)))
    slot_grad = jnp.zeros((slot_total, row_width), jnp.float32).at[slot_ids].add(conj_product(query_grads, word_used.astype(jnp.float32)))
    slot_grad = slot_grad + 0.02 * live_mask[:, None] * slot_table.astype(jnp.float32)
    return word_part, ctx_part, relation_ids, slot_grad


def reference(words, contexts, relations, word_index, context_index, rel_slot, neg_index, requests, counts):
    row_width = 2 * RANK
    word_blocks = words.reshape(ENT_PARTS, PART, row_width)
    held_blocks = jnp.roll(contexts.reshape(ENT_PARTS, PART, row_width), 1, axis=0)
    word_ids = word_index.reshape(ENT_PARTS, REL_SPLIT, TRIPS)
    ctx_ids = context_index.reshape(ENT_PARTS, REL_SPLIT, TRIPS)
    slot_ids = rel_slot.reshape(ENT_PARTS, REL_SPLIT, TRIPS)
    neg_ids = neg_index.reshape(ENT_PARTS, REL_SPLIT, BLOCKS, NEG)
    wanted = requests.reshape(ENT_PARTS, REL_SPLIT, OWNERS * SLOTS)
    live_counts = counts.reshape(ENT_PARTS, REL_SPLIT, OWNERS)

    def per_block(rel_total, inputs_one):
        word_rows, held_rows, wids, cids, sids, nids, wants, lives = inputs_one
        word_sum = jnp.zeros((PART, row_width), jnp.float32)
        ctx_sum = jnp.zeros((PART, row_width), jnp.float32)
        for half_index in range(REL_SPLIT):
            word_part, ctx_part, relation_ids, slot_grad = one_device(relations, word_rows, held_rows, wids[half_index], cids[half_index], sids[half_index], nids[half_index], wants[half_index], lives[half_index])
            word_sum = word_sum + lax.optimization_barrier(word_part.astype(jnp.bfloat16)).astype(jnp.float32)
            ctx_sum = ctx_sum + lax.optimization_barrier(ctx_part.astype(jnp.bfloat16)).astype(jnp.float32)
            rel_total = rel_total.at[relation_ids].add(slot_grad)
        return rel_total, (word_sum.astype(jnp.bfloat16), ctx_sum.astype(jnp.bfloat16))

    rel_total, outputs = lax.scan(per_block, jnp.zeros((NREL, row_width), jnp.float32), (word_blocks, held_blocks, word_ids, ctx_ids, slot_ids, neg_ids, wanted, live_counts))
    word_out, ctx_out = outputs
    return word_out.reshape(NWORD, row_width), ctx_out.reshape(NWORD, row_width), rel_total
```

```python
import jax
import jax.numpy as jnp
from jax import lax
from jax.sharding import PartitionSpec as P


def passed_along(shard, axis, by):
    length = lax.axis_size(axis)
    return lax.ppermute(shard, axis, [(i, (i + by) % length) for i in range(length)])


def complex_product(left_vec, right_vec, half_width):
    left_re, left_im = (left_vec[:, :half_width], left_vec[:, half_width:])
    right_re, right_im = (right_vec[:, :half_width], right_vec[:, half_width:])
    return jnp.concatenate(
        [left_re * right_re - left_im * right_im, left_re * right_im + left_im * right_re], axis=1
    )


def conj_product(grad_vec, other_vec, half_width):
    grad_re, grad_im = (grad_vec[:, :half_width], grad_vec[:, half_width:])
    other_re, other_im = (other_vec[:, :half_width], other_vec[:, half_width:])
    return jnp.concatenate(
        [grad_re * other_re + grad_im * other_im, grad_im * other_re - grad_re * other_im], axis=1
    )


def one_hot_rows(index_ids, row_total):
    return (jnp.arange(row_total)[:, None] == index_ids[None, :]).astype(jnp.bfloat16)


def spread_rows(selector, terms):
    upper = terms.astype(jnp.bfloat16)
    lower = (terms - upper.astype(jnp.float32)).astype(jnp.bfloat16)
    return jnp.dot(selector, upper, preferred_element_type=jnp.float32) + jnp.dot(
        selector, lower, preferred_element_type=jnp.float32
    )


def shards(
    words, contexts, relations, word_index, context_index, rel_slot, neg_index, requests, counts
):
    row_width = words.shape[1]
    half_width = row_width // 2
    part_count = lax.axis_size("blk")
    split_count = lax.axis_size("rel")
    slot_count = requests.shape[-1]
    owned_rows = relations.shape[0]
    block_count = neg_index.shape[0]
    block_size = word_index.shape[0] // block_count
    part_rows = contexts.shape[0]
    neg_scale = float(neg_index.shape[1]) ** (-0.5)
    held_rows = passed_along(contexts, "blk", 1)
    wanted = requests[0, 0].reshape(part_count * split_count, slot_count)
    both = ("blk", "rel")
    incoming = lax.all_to_all(wanted, both, split_axis=0, concat_axis=0, tiled=True)
    picked = relations[incoming.reshape(-1)].reshape(part_count * split_count, slot_count, row_width)
    fetched = lax.all_to_all(picked, both, split_axis=0, concat_axis=0, tiled=True)
    slot_table = fetched.reshape(-1, row_width)
    slot_total = slot_table.shape[0]
    live_mask = (
        (jnp.arange(slot_count)[None, None, :] < counts[0, 0][:, :, None])
        .reshape(-1)
        .astype(jnp.float32)
    )
    word_used = words[word_index]
    ctx_used = held_rows[context_index]
    rel_used = slot_table[rel_slot]
    query = complex_product(
        word_used.astype(jnp.float32), rel_used.astype(jnp.float32), half_width
    ).astype(jnp.bfloat16)
    positive = jnp.einsum("td,td->t", query, ctx_used, preferred_element_type=jnp.float32)
    pos_grad = -jax.nn.sigmoid(-positive)
    ctx_start = spread_rows(
        one_hot_rows(context_index, part_rows), pos_grad[:, None] * query.astype(jnp.float32)
    )

    def block_step(ctx_total, inputs_one):
        query_block, ctx_block, neg_block, pos_block = inputs_one
        selector = one_hot_rows(neg_block, part_rows)
        neg_rows = lax.dot_general(
            selector, held_rows, (((0,), (0,)), ((), ())), preferred_element_type=jnp.float32
        ).astype(jnp.bfloat16)
        scores = lax.dot_general(
            query_block, neg_rows, (((1,), (1,)), ((), ())), preferred_element_type=jnp.float32
        )
        neg_grad = (jax.nn.sigmoid(scores) * neg_scale).astype(jnp.bfloat16)
        query_grad = pos_block[:, None] * ctx_block.astype(jnp.float32) + jnp.dot(
            neg_grad, neg_rows, preferred_element_type=jnp.float32
        )
        back_rows = lax.dot_general(
            neg_grad, query_block, (((0,), (0,)), ((), ())), preferred_element_type=jnp.float32
        )
        return (ctx_total + spread_rows(selector, back_rows), query_grad)

    ctx_part, query_grads = lax.scan(
        block_step,
        ctx_start,
        (
            query.reshape(block_count, block_size, row_width),
            ctx_used.reshape(block_count, block_size, row_width),
            neg_index,
            pos_grad.reshape(block_count, block_size),
        ),
    )
    query_grads = query_grads.reshape(-1, row_width)
    word_part = spread_rows(
        one_hot_rows(word_index, words.shape[0]),
        conj_product(query_grads, rel_used.astype(jnp.float32), half_width),
    )
    slot_grad = spread_rows(
        one_hot_rows(rel_slot, slot_total),
        conj_product(query_grads, word_used.astype(jnp.float32), half_width),
    )
    slot_grad = slot_grad + 0.02 * live_mask[:, None] * slot_table.astype(jnp.float32)
    word_half = word_part.astype(jnp.bfloat16)
    ctx_half = ctx_part.astype(jnp.bfloat16)
    word_sum = word_half.astype(jnp.float32) + passed_along(word_half, "rel", 1).astype(jnp.float32)
    ctx_sum = ctx_half.astype(jnp.float32) + passed_along(ctx_half, "rel", 1).astype(jnp.float32)
    outgoing = slot_grad.reshape(part_count * split_count, slot_count, row_width)
    returned = lax.all_to_all(
        outgoing.astype(jnp.bfloat16), both, split_axis=0, concat_axis=0, tiled=True
    ).astype(outgoing.dtype)
    owner_map = (incoming.reshape(-1)[None, :] == jnp.arange(owned_rows)[:, None]).astype(
        jnp.float32
    )
    relation_grad = jnp.dot(
        owner_map,
        returned.reshape(-1, row_width),
        precision=lax.Precision.HIGHEST,
        preferred_element_type=jnp.float32,
    )
    return (word_sum.astype(jnp.bfloat16), ctx_sum.astype(jnp.bfloat16), relation_grad)


def solution(mesh):
    return jax.shard_map(
        shards,
        mesh=mesh,
        in_specs=(
            P("blk", None),
            P("blk", None),
            P(("blk", "rel"), None),
            P(("blk", "rel")),
            P(("blk", "rel")),
            P(("blk", "rel")),
            P(("blk", "rel"), None),
            P("blk", "rel", None, None, None),
            P("blk", "rel", None, None),
        ),
        out_specs=(P("blk", None), P("blk", None), P(("blk", "rel"), None)),
        check_vma=False,
    )
```

```python
import jax
import jax.numpy as jnp
from jax import lax
from jax.sharding import PartitionSpec as P


def passed_along(shard, axis, by):
    length = lax.axis_size(axis)
    return lax.ppermute(shard, axis, [(i, (i + by) % length) for i in range(length)])


def complex_product(left_vec, right_vec, half_width):
    left_re, left_im = (left_vec[..., :half_width], left_vec[..., half_width:])
    right_re, right_im = (right_vec[..., :half_width], right_vec[..., half_width:])
    return jnp.concatenate(
        [left_re * right_re - left_im * right_im, left_re * right_im + left_im * right_re], axis=-1
    )


def conj_product(grad_vec, other_vec, half_width):
    grad_re, grad_im = (grad_vec[..., :half_width], grad_vec[..., half_width:])
    other_re, other_im = (other_vec[..., :half_width], other_vec[..., half_width:])
    return jnp.concatenate(
        [grad_re * other_re + grad_im * other_im, grad_im * other_re - grad_re * other_im], axis=-1
    )


def one_hot(index_ids, row_total):
    return (index_ids[..., None] == jnp.arange(row_total)).astype(jnp.bfloat16)


def pick_rows(selector, rows):
    return jnp.dot(selector, rows, preferred_element_type=jnp.float32)


def split_bf16(values):
    upper = values.astype(jnp.bfloat16)
    lower = (values - upper.astype(jnp.float32)).astype(jnp.bfloat16)
    return upper, lower


def spread_rows(selector, terms):
    upper, lower = split_bf16(terms)
    dims = (((0,), (0,)), ((), ()))
    return lax.dot_general(
        selector, upper, dims, preferred_element_type=jnp.float32
    ) + lax.dot_general(selector, lower, dims, preferred_element_type=jnp.float32)


def shards(
    words, contexts, relations, word_index, context_index, rel_slot, neg_index, requests, counts
):
    row_width = words.shape[1]
    half_width = row_width // 2
    part_count = lax.axis_size("blk")
    split_count = lax.axis_size("rel")
    owner_count = part_count * split_count
    slot_count = requests.shape[-1]
    slot_total = owner_count * slot_count
    owned_rows = relations.shape[0]
    part_rows = contexts.shape[0]
    trips = word_index.shape[0]
    block_count = neg_index.shape[0]
    neg_count = neg_index.shape[1]
    block_size = trips // block_count
    neg_scale = float(neg_count) ** (-0.5)
    both = ("blk", "rel")

    held_rows = passed_along(contexts, "blk", 1)

    own_ints = jnp.concatenate([word_index, context_index, rel_slot, neg_index.reshape(-1)])
    bucket_ints = jnp.stack(
        [own_ints] + [passed_along(own_ints, "rel", -j) for j in range(1, split_count)]
    )
    word_ids = bucket_ints[:, :trips].reshape(-1)
    ctx_ids = bucket_ints[:, trips : 2 * trips].reshape(-1)
    slot_ids = (
        bucket_ints[:, 2 * trips : 3 * trips] + (jnp.arange(split_count) * slot_total)[:, None]
    ).reshape(-1)
    neg_ids = bucket_ints[:, 3 * trips :].reshape(split_count * block_count, neg_count)

    wanted = requests[0, 0].reshape(owner_count, slot_count)
    incoming = lax.all_to_all(wanted, both, split_axis=0, concat_axis=0, tiled=True)
    requester = jnp.arange(owner_count)
    bucket_of = (requester // split_count) * split_count
    served = jnp.stack(
        [incoming[bucket_of + (requester + j) % split_count] for j in range(split_count)], axis=1
    )
    picked = relations[served.reshape(-1)].reshape(
        owner_count, split_count * slot_count, row_width
    )
    fetched = lax.all_to_all(picked, both, split_axis=0, concat_axis=0, tiled=True)
    slot_table = (
        fetched.reshape(owner_count, split_count, slot_count, row_width)
        .transpose(1, 0, 2, 3)
        .reshape(split_count * slot_total, row_width)
    )
    own_table = slot_table[:slot_total]
    live_mask = (
        (jnp.arange(slot_count)[None, :] < counts[0, 0].reshape(owner_count)[:, None])
        .reshape(-1)
        .astype(jnp.float32)
    )

    word_sel = one_hot(word_ids, part_rows)
    ctx_sel = one_hot(ctx_ids, part_rows)
    word_used = pick_rows(word_sel, words)
    ctx_used = pick_rows(ctx_sel, held_rows)
    rel_used = pick_rows(one_hot(slot_ids, split_count * slot_total), slot_table)
    query = complex_product(word_used, rel_used, half_width).astype(jnp.bfloat16)
    positive = jnp.sum(query.astype(jnp.float32) * ctx_used, axis=1)
    pos_grad = -jax.nn.sigmoid(-positive)

    group_count = split_count * block_count
    query_blocks = query.reshape(group_count, block_size, row_width)
    neg_sel = one_hot(neg_ids, part_rows)
    neg_rows = jnp.einsum(
        "gjp,pd->gjd", neg_sel, held_rows, preferred_element_type=jnp.float32
    ).astype(jnp.bfloat16)
    scores = jnp.einsum(
        "gtd,gjd->gtj", query_blocks, neg_rows, preferred_element_type=jnp.float32
    )
    neg_grad = (jax.nn.sigmoid(scores) * neg_scale).astype(jnp.bfloat16)
    pos_blocks = pos_grad.reshape(group_count, block_size)
    query_grads = pos_blocks[:, :, None] * ctx_used.reshape(
        group_count, block_size, row_width
    ) + jnp.einsum("gtj,gjd->gtd", neg_grad, neg_rows, preferred_element_type=jnp.float32)

    neg_weight = jnp.einsum("gtj,gjp->gpt", neg_grad, neg_sel, preferred_element_type=jnp.float32)
    pos_weight = jnp.where(
        ctx_ids.reshape(group_count, 1, block_size)
        == jnp.arange(part_rows)[None, :, None],
        pos_blocks[:, None, :],
        0.0,
    )
    weight_hi, weight_lo = split_bf16(neg_weight + pos_weight)
    ctx_sum = jnp.einsum(
        "gpt,gtd->pd", weight_hi, query_blocks, preferred_element_type=jnp.float32
    ) + jnp.einsum("gpt,gtd->pd", weight_lo, query_blocks, preferred_element_type=jnp.float32)

    query_grads = query_grads.reshape(-1, row_width)
    word_sum = spread_rows(word_sel, conj_product(query_grads, rel_used, half_width))
    slot_grad = spread_rows(
        one_hot(slot_ids[:trips], slot_total),
        conj_product(query_grads[:trips], word_used[:trips], half_width),
    )
    slot_grad = slot_grad + 0.02 * live_mask[:, None] * own_table.astype(jnp.float32)
    outgoing = slot_grad.reshape(owner_count, slot_count, row_width)
    returned = lax.all_to_all(
        outgoing.astype(jnp.bfloat16), both, split_axis=0, concat_axis=0, tiled=True
    ).astype(outgoing.dtype)
    owner_map = (incoming.reshape(-1)[None, :] == jnp.arange(owned_rows)[:, None]).astype(
        jnp.float32
    )
    relation_grad = jnp.dot(
        owner_map,
        returned.reshape(-1, row_width),
        precision=lax.Precision.HIGHEST,
        preferred_element_type=jnp.float32,
    )
    return (word_sum.astype(jnp.bfloat16), ctx_sum.astype(jnp.bfloat16), relation_grad)


def solution(mesh):
    return jax.shard_map(
        shards,
        mesh=mesh,
        in_specs=(
            P("blk", None),
            P("blk", None),
            P(("blk", "rel"), None),
            P(("blk", "rel")),
            P(("blk", "rel")),
            P(("blk", "rel")),
            P(("blk", "rel"), None),
            P("blk", "rel", None, None, None),
            P("blk", "rel", None, None),
        ),
        out_specs=(P("blk", None), P("blk", None), P(("blk", "rel"), None)),
        check_vma=False,
    )
```

```python
import jax
import jax.numpy as jnp
from jax import lax
from jax.sharding import PartitionSpec as P


def passed_along(shard, axis, by):
    length = lax.axis_size(axis)
    return lax.ppermute(shard, axis, [(i, (i + by) % length) for i in range(length)])


def complex_product(left_vec, right_vec, half_width):
    left_re, left_im = (left_vec[..., :half_width], left_vec[..., half_width:])
    right_re, right_im = (right_vec[..., :half_width], right_vec[..., half_width:])
    return jnp.concatenate(
        [left_re * right_re - left_im * right_im, left_re * right_im + left_im * right_re], axis=-1
    )


def conj_product(grad_vec, other_vec, half_width):
    grad_re, grad_im = (grad_vec[..., :half_width], grad_vec[..., half_width:])
    other_re, other_im = (other_vec[..., :half_width], other_vec[..., half_width:])
    return jnp.concatenate(
        [grad_re * other_re + grad_im * other_im, grad_im * other_re - grad_re * other_im], axis=-1
    )


def one_hot(index_ids, row_total):
    return (index_ids[..., None] == jnp.arange(row_total)).astype(jnp.bfloat16)


def pick_rows(selector, rows):
    return jnp.dot(selector, rows, preferred_element_type=jnp.float32)


def split_bf16(values):
    upper = values.astype(jnp.bfloat16)
    lower = (values - upper.astype(jnp.float32)).astype(jnp.bfloat16)
    return upper, lower


def spread_rows(selector, terms):
    upper, lower = split_bf16(terms)
    dims = (((0,), (0,)), ((), ()))
    return lax.dot_general(
        selector, upper, dims, preferred_element_type=jnp.float32
    ) + lax.dot_general(selector, lower, dims, preferred_element_type=jnp.float32)


def shards(
    words, contexts, relations, word_index, context_index, rel_slot, neg_index, requests, counts
):
    row_width = words.shape[1]
    half_width = row_width // 2
    part_count = lax.axis_size("blk")
    split_count = lax.axis_size("rel")
    owner_count = part_count * split_count
    slot_count = requests.shape[-1]
    slot_total = owner_count * slot_count
    owned_rows = relations.shape[0]
    part_rows = contexts.shape[0]
    trips = word_index.shape[0]
    block_count = neg_index.shape[0]
    neg_count = neg_index.shape[1]
    block_size = trips // block_count
    neg_scale = float(neg_count) ** (-0.5)
    both = ("blk", "rel")

    held_rows = passed_along(contexts, "blk", 1)

    own_ints = jnp.concatenate([word_index, context_index, rel_slot, neg_index.reshape(-1)])
    bucket_ints = jnp.stack(
        [own_ints] + [passed_along(own_ints, "rel", -j) for j in range(1, split_count)]
    )
    word_ids = bucket_ints[:, :trips].reshape(-1)
    ctx_ids = bucket_ints[:, trips : 2 * trips].reshape(-1)
    slot_ids = (
        bucket_ints[:, 2 * trips : 3 * trips] + (jnp.arange(split_count) * slot_total)[:, None]
    ).reshape(-1)
    neg_ids = bucket_ints[:, 3 * trips :].reshape(split_count * block_count, neg_count)

    wanted = requests[0, 0].reshape(owner_count, slot_count)
    incoming = lax.all_to_all(wanted, both, split_axis=0, concat_axis=0, tiled=True)
    requester = jnp.arange(owner_count)
    bucket_of = (requester // split_count) * split_count
    served = jnp.stack(
        [incoming[bucket_of + (requester + j) % split_count] for j in range(split_count)], axis=1
    )
    picked = pick_rows(one_hot(served.reshape(-1), owned_rows), relations).astype(
        jnp.bfloat16
    ).reshape(owner_count, split_count * slot_count, row_width)
    fetched = lax.all_to_all(picked, both, split_axis=0, concat_axis=0, tiled=True)
    slot_table = (
        fetched.reshape(owner_count, split_count, slot_count, row_width)
        .transpose(1, 0, 2, 3)
        .reshape(split_count * slot_total, row_width)
    )
    own_table = slot_table[:slot_total]
    live_mask = (
        (jnp.arange(slot_count)[None, :] < counts[0, 0].reshape(owner_count)[:, None])
        .reshape(-1)
        .astype(jnp.float32)
    )

    group_count = split_count * block_count
    slot_sel = one_hot(slot_ids, split_count * slot_total)
    word_sum = jnp.zeros((part_rows, row_width), jnp.float32)
    ctx_sum = jnp.zeros((part_rows, row_width), jnp.float32)
    slot_grad = jnp.zeros((slot_total, row_width), jnp.float32)
    for group in range(group_count):
        rows_of = slice(group * block_size, (group + 1) * block_size)
        word_sel = one_hot(word_ids[rows_of], part_rows)
        ctx_ids_of = ctx_ids[rows_of]
        word_used = pick_rows(word_sel, words)
        ctx_used = pick_rows(one_hot(ctx_ids_of, part_rows), held_rows)
        rel_used = pick_rows(slot_sel[rows_of], slot_table)
        query = complex_product(word_used, rel_used, half_width).astype(jnp.bfloat16)
        positive = jnp.sum(query.astype(jnp.float32) * ctx_used, axis=1)
        pos_grad = -jax.nn.sigmoid(-positive)
        neg_sel = one_hot(neg_ids[group], part_rows)
        neg_rows = pick_rows(neg_sel, held_rows).astype(jnp.bfloat16)
        scores = lax.dot_general(
            query, neg_rows, (((1,), (1,)), ((), ())), preferred_element_type=jnp.float32
        )
        neg_grad = (jax.nn.sigmoid(scores) * neg_scale).astype(jnp.bfloat16)
        query_grad = pos_grad[:, None] * ctx_used + jnp.dot(
            neg_grad, neg_rows, preferred_element_type=jnp.float32
        )
        if group < block_count:
            slot_grad = slot_grad + spread_rows(
                one_hot(slot_ids[rows_of], slot_total),
                conj_product(query_grad, word_used, half_width),
            )
        neg_weight = lax.dot_general(
            neg_sel, neg_grad, (((0,), (1,)), ((), ())), preferred_element_type=jnp.float32
        )
        pos_weight = jnp.where(
            ctx_ids_of[None, :] == jnp.arange(part_rows)[:, None], pos_grad[None, :], 0.0
        )
        weight_hi, weight_lo = split_bf16(neg_weight + pos_weight)
        ctx_sum = (
            ctx_sum
            + jnp.dot(weight_hi, query, preferred_element_type=jnp.float32)
            + jnp.dot(weight_lo, query, preferred_element_type=jnp.float32)
        )
        word_sum = word_sum + spread_rows(
            word_sel, conj_product(query_grad, rel_used, half_width)
        )
    slot_grad = slot_grad + 0.02 * live_mask[:, None] * own_table.astype(jnp.float32)
    outgoing = slot_grad.reshape(owner_count, slot_count, row_width)
    returned = lax.all_to_all(
        outgoing.astype(jnp.bfloat16), both, split_axis=0, concat_axis=0, tiled=True
    ).astype(outgoing.dtype)
    owner_map = (incoming.reshape(-1)[None, :] == jnp.arange(owned_rows)[:, None]).astype(
        jnp.float32
    )
    relation_grad = jnp.dot(
        owner_map,
        returned.reshape(-1, row_width),
        precision=lax.Precision.HIGHEST,
        preferred_element_type=jnp.float32,
    )
    return (word_sum.astype(jnp.bfloat16), ctx_sum.astype(jnp.bfloat16), relation_grad)


def solution(mesh):
    return jax.shard_map(
        shards,
        mesh=mesh,
        in_specs=(
            P("blk", None),
            P("blk", None),
            P(("blk", "rel"), None),
            P(("blk", "rel")),
            P(("blk", "rel")),
            P(("blk", "rel")),
            P(("blk", "rel"), None),
            P("blk", "rel", None, None, None),
            P("blk", "rel", None, None),
        ),
        out_specs=(P("blk", None), P("blk", None), P(("blk", "rel"), None)),
        check_vma=False,
    )
```

```python
import jax
import jax.numpy as jnp
from jax import lax
from jax.sharding import PartitionSpec as P


def passed_along(shard, axis, by):
    length = lax.axis_size(axis)
    return lax.ppermute(shard, axis, [(i, (i + by) % length) for i in range(length)])


def complex_product(left_vec, right_vec, half_width):
    left_re, left_im = (left_vec[..., :half_width], left_vec[..., half_width:])
    right_re, right_im = (right_vec[..., :half_width], right_vec[..., half_width:])
    return jnp.concatenate(
        [left_re * right_re - left_im * right_im, left_re * right_im + left_im * right_re], axis=-1
    )


def conj_product(grad_vec, other_vec, half_width):
    grad_re, grad_im = (grad_vec[..., :half_width], grad_vec[..., half_width:])
    other_re, other_im = (other_vec[..., :half_width], other_vec[..., half_width:])
    return jnp.concatenate(
        [grad_re * other_re + grad_im * other_im, grad_im * other_re - grad_re * other_im], axis=-1
    )


def one_hot(index_ids, row_total):
    return (index_ids[..., None] == jnp.arange(row_total)).astype(jnp.bfloat16)


def pick_rows(selector, rows):
    return jnp.dot(selector, rows, preferred_element_type=jnp.float32)


def split_bf16(values):
    upper = values.astype(jnp.bfloat16)
    lower = (values - upper.astype(jnp.float32)).astype(jnp.bfloat16)
    return upper, lower


def spread_rows(selector, terms):
    upper, lower = split_bf16(terms)
    dims = (((0,), (0,)), ((), ()))
    return lax.dot_general(
        selector, upper, dims, preferred_element_type=jnp.float32
    ) + lax.dot_general(selector, lower, dims, preferred_element_type=jnp.float32)


def shards(
    words, contexts, relations, word_index, context_index, rel_slot, neg_index, requests, counts
):
    row_width = words.shape[1]
    half_width = row_width // 2
    part_count = lax.axis_size("blk")
    split_count = lax.axis_size("rel")
    owner_count = part_count * split_count
    slot_count = requests.shape[-1]
    slot_total = owner_count * slot_count
    owned_rows = relations.shape[0]
    part_rows = contexts.shape[0]
    trips = word_index.shape[0]
    block_count = neg_index.shape[0]
    neg_count = neg_index.shape[1]
    block_size = trips // block_count
    neg_scale = float(neg_count) ** (-0.5)
    both = ("blk", "rel")

    held_rows = passed_along(contexts, "blk", 1)

    own_ints = jnp.concatenate([word_index, context_index, rel_slot, neg_index.reshape(-1)])
    bucket_ints = jnp.stack(
        [own_ints] + [passed_along(own_ints, "rel", -j) for j in range(1, split_count)]
    )
    word_ids = bucket_ints[:, :trips].reshape(-1)
    ctx_ids = bucket_ints[:, trips : 2 * trips].reshape(-1)
    slot_ids = (
        bucket_ints[:, 2 * trips : 3 * trips] + (jnp.arange(split_count) * slot_total)[:, None]
    ).reshape(-1)
    neg_ids = bucket_ints[:, 3 * trips :].reshape(split_count * block_count, neg_count)

    wanted = requests[0, 0].reshape(owner_count, slot_count)
    incoming = lax.all_to_all(wanted, both, split_axis=0, concat_axis=0, tiled=True)
    lists = incoming.reshape(part_count, split_count, slot_count)
    served = jnp.stack([jnp.roll(lists, -j, axis=1) for j in range(split_count)], axis=2)
    picked = pick_rows(one_hot(served.reshape(-1), owned_rows), relations).astype(
        jnp.bfloat16
    ).reshape(owner_count, split_count * slot_count, row_width)
    fetched = lax.all_to_all(picked, both, split_axis=0, concat_axis=0, tiled=True)
    live_mask = (
        (jnp.arange(slot_count)[None, :] < counts[0, 0].reshape(owner_count)[:, None])
        .reshape(-1)
        .astype(jnp.float32)
    )

    group_count = split_count * block_count
    word_sel = one_hot(word_ids, part_rows)
    ctx_sel = one_hot(ctx_ids, part_rows)
    neg_sel = one_hot(neg_ids, part_rows)
    word_used = pick_rows(word_sel, words)
    ctx_used = pick_rows(ctx_sel, held_rows)
    neg_rows = jnp.einsum(
        "gjp,pd->gjd", neg_sel, held_rows, preferred_element_type=jnp.float32
    ).astype(jnp.bfloat16)
    fetched, word_used, ctx_used, neg_rows = lax.optimization_barrier(
        (fetched, word_used, ctx_used, neg_rows)
    )
    slot_table = (
        fetched.reshape(owner_count, split_count, slot_count, row_width)
        .transpose(1, 0, 2, 3)
        .reshape(split_count * slot_total, row_width)
    )
    own_table = slot_table[:slot_total]
    rel_used = pick_rows(one_hot(slot_ids, split_count * slot_total), slot_table)
    query = complex_product(word_used, rel_used, half_width).astype(jnp.bfloat16)
    positive = jnp.sum(query.astype(jnp.float32) * ctx_used, axis=1)
    pos_grad = -jax.nn.sigmoid(-positive)
    query_blocks = query.reshape(group_count, block_size, row_width)
    scores = jnp.einsum(
        "gtd,gjd->gtj", query_blocks, neg_rows, preferred_element_type=jnp.float32
    )
    neg_grad = (jax.nn.sigmoid(scores) * neg_scale).astype(jnp.bfloat16)
    pos_blocks = pos_grad.reshape(group_count, block_size)
    query_grads = (
        pos_blocks[:, :, None] * ctx_used.reshape(group_count, block_size, row_width)
        + jnp.einsum("gtj,gjd->gtd", neg_grad, neg_rows, preferred_element_type=jnp.float32)
    ).reshape(-1, row_width)
    slot_grad = spread_rows(
        one_hot(slot_ids[:trips], slot_total),
        conj_product(query_grads[:trips], word_used[:trips], half_width),
    )

    neg_weight = jnp.einsum("gtj,gjp->gpt", neg_grad, neg_sel, preferred_element_type=jnp.float32)
    pos_weight = jnp.where(
        ctx_ids.reshape(group_count, 1, block_size) == jnp.arange(part_rows)[None, :, None],
        pos_blocks[:, None, :],
        0.0,
    )
    weight_hi, weight_lo = split_bf16(neg_weight + pos_weight)
    ctx_sum = jnp.einsum(
        "gpt,gtd->pd", weight_hi, query_blocks, preferred_element_type=jnp.float32
    ) + jnp.einsum("gpt,gtd->pd", weight_lo, query_blocks, preferred_element_type=jnp.float32)
    word_sum = spread_rows(word_sel, conj_product(query_grads, rel_used, half_width))
    slot_grad = slot_grad + 0.02 * live_mask[:, None] * own_table.astype(jnp.float32)
    outgoing = slot_grad.reshape(owner_count, slot_count, row_width)
    returned = lax.all_to_all(
        outgoing.astype(jnp.bfloat16), both, split_axis=0, concat_axis=0, tiled=True
    ).astype(outgoing.dtype)
    owner_map = (incoming.reshape(-1)[None, :] == jnp.arange(owned_rows)[:, None]).astype(
        jnp.float32
    )
    relation_grad = jnp.dot(
        owner_map,
        returned.reshape(-1, row_width),
        precision=lax.Precision.HIGHEST,
        preferred_element_type=jnp.float32,
    )
    return (word_sum.astype(jnp.bfloat16), ctx_sum.astype(jnp.bfloat16), relation_grad)


def solution(mesh):
    return jax.shard_map(
        shards,
        mesh=mesh,
        in_specs=(
            P("blk", None),
            P("blk", None),
            P(("blk", "rel"), None),
            P(("blk", "rel")),
            P(("blk", "rel")),
            P(("blk", "rel")),
            P(("blk", "rel"), None),
            P("blk", "rel", None, None, None),
            P("blk", "rel", None, None),
        ),
        out_specs=(P("blk", None), P("blk", None), P(("blk", "rel"), None)),
        check_vma=False,
    )
```

```python
import jax
import jax.numpy as jnp
from jax import lax
from jax.sharding import PartitionSpec as P


def passed_along(shard, axis, by):
    length = lax.axis_size(axis)
    return lax.ppermute(shard, axis, [(i, (i + by) % length) for i in range(length)])


def complex_product(left_vec, right_vec, half_width):
    left_re, left_im = (left_vec[..., :half_width], left_vec[..., half_width:])
    right_re, right_im = (right_vec[..., :half_width], right_vec[..., half_width:])
    return jnp.concatenate(
        [left_re * right_re - left_im * right_im, left_re * right_im + left_im * right_re], axis=-1
    )


def conj_product(grad_vec, other_vec, half_width):
    grad_re, grad_im = (grad_vec[..., :half_width], grad_vec[..., half_width:])
    other_re, other_im = (other_vec[..., :half_width], other_vec[..., half_width:])
    return jnp.concatenate(
        [grad_re * other_re + grad_im * other_im, grad_im * other_re - grad_re * other_im], axis=-1
    )


def one_hot(index_ids, row_total):
    return (index_ids[..., None] == jnp.arange(row_total)).astype(jnp.bfloat16)


def pick_rows(selector, rows):
    return jnp.dot(selector, rows, preferred_element_type=jnp.float32)


def split_bf16(values):
    upper = values.astype(jnp.bfloat16)
    lower = (values - upper.astype(jnp.float32)).astype(jnp.bfloat16)
    return upper, lower


def spread_rows(selector, terms):
    upper, lower = split_bf16(terms)
    dims = (((0,), (0,)), ((), ()))
    return lax.dot_general(
        selector, upper, dims, preferred_element_type=jnp.float32
    ) + lax.dot_general(selector, lower, dims, preferred_element_type=jnp.float32)


def shards(
    words, contexts, relations, word_index, context_index, rel_slot, neg_index, requests, counts
):
    row_width = words.shape[1]
    half_width = row_width // 2
    part_count = lax.axis_size("blk")
    split_count = lax.axis_size("rel")
    owner_count = part_count * split_count
    slot_count = requests.shape[-1]
    slot_total = owner_count * slot_count
    owned_rows = relations.shape[0]
    part_rows = contexts.shape[0]
    trips = word_index.shape[0]
    block_count = neg_index.shape[0]
    neg_count = neg_index.shape[1]
    block_size = trips // block_count
    neg_scale = float(neg_count) ** (-0.5)
    both = ("blk", "rel")

    held_rows = passed_along(contexts, "blk", 1)

    own_ints = jnp.concatenate([word_index, context_index, rel_slot, neg_index.reshape(-1)])
    bucket_ints = jnp.stack(
        [own_ints] + [passed_along(own_ints, "rel", -j) for j in range(1, split_count)]
    )
    word_ids = bucket_ints[:, :trips].reshape(-1)
    ctx_ids = bucket_ints[:, trips : 2 * trips].reshape(-1)
    slot_ids = (
        bucket_ints[:, 2 * trips : 3 * trips] + (jnp.arange(split_count) * slot_total)[:, None]
    ).reshape(-1)
    neg_ids = bucket_ints[:, 3 * trips :].reshape(split_count * block_count, neg_count)

    wanted = requests[0, 0].reshape(owner_count, slot_count)
    incoming = lax.all_to_all(wanted, both, split_axis=0, concat_axis=0, tiled=True)
    lists = incoming.reshape(part_count, split_count, slot_count)
    served = jnp.stack([jnp.roll(lists, -j, axis=1) for j in range(split_count)], axis=2)
    picked = pick_rows(one_hot(served.reshape(-1), owned_rows), relations).astype(
        jnp.bfloat16
    ).reshape(owner_count, split_count * slot_count, row_width)
    fetched = lax.all_to_all(picked, both, split_axis=0, concat_axis=0, tiled=True)
    live_mask = (
        (jnp.arange(slot_count)[None, :] < counts[0, 0].reshape(owner_count)[:, None])
        .reshape(-1)
        .astype(jnp.float32)
    )

    group_count = split_count * block_count
    word_sel = one_hot(word_ids, part_rows)
    ctx_sel = one_hot(ctx_ids, part_rows)
    neg_sel = one_hot(neg_ids, part_rows)
    word_used = pick_rows(word_sel, words)
    ctx_used = pick_rows(ctx_sel, held_rows)
    neg_rows = jnp.einsum(
        "gjp,pd->gjd", neg_sel, held_rows, preferred_element_type=jnp.float32
    ).astype(jnp.bfloat16)
    fetched, word_used, ctx_used, neg_rows = lax.optimization_barrier(
        (fetched, word_used, ctx_used, neg_rows)
    )
    slot_table = (
        fetched.reshape(owner_count, split_count, slot_count, row_width)
        .transpose(1, 0, 2, 3)
        .reshape(split_count * slot_total, row_width)
    )
    own_table = slot_table[:slot_total]
    rel_used = pick_rows(one_hot(slot_ids, split_count * slot_total), slot_table)
    word_blocks = word_used.reshape(group_count, block_size, row_width)
    ctx_blocks = ctx_used.reshape(group_count, block_size, row_width)
    rel_blocks = rel_used.reshape(group_count, block_size, row_width)

    def block_chain(group):
        query = complex_product(word_blocks[group], rel_blocks[group], half_width).astype(
            jnp.bfloat16
        )
        positive = jnp.sum(query.astype(jnp.float32) * ctx_blocks[group], axis=1)
        pos_grad = -jax.nn.sigmoid(-positive)
        scores = lax.dot_general(
            query, neg_rows[group], (((1,), (1,)), ((), ())), preferred_element_type=jnp.float32
        )
        neg_grad = (jax.nn.sigmoid(scores) * neg_scale).astype(jnp.bfloat16)
        query_grad = pos_grad[:, None] * ctx_blocks[group] + jnp.dot(
            neg_grad, neg_rows[group], preferred_element_type=jnp.float32
        )
        return query, pos_grad, neg_grad, query_grad

    chains = [block_chain(group) for group in range(block_count)]
    own_grads = jnp.concatenate([chain[3] for chain in chains])
    slot_grad = spread_rows(
        one_hot(slot_ids[:trips], slot_total),
        conj_product(own_grads, word_used[:trips], half_width),
    )
    chains += [block_chain(group) for group in range(block_count, group_count)]
    query_blocks = jnp.stack([chain[0] for chain in chains])
    pos_blocks = jnp.stack([chain[1] for chain in chains])
    neg_grad = jnp.stack([chain[2] for chain in chains])
    query_grads = jnp.concatenate([chain[3] for chain in chains])

    neg_weight = jnp.einsum("gtj,gjp->gpt", neg_grad, neg_sel, preferred_element_type=jnp.float32)
    pos_weight = jnp.where(
        ctx_ids.reshape(group_count, 1, block_size) == jnp.arange(part_rows)[None, :, None],
        pos_blocks[:, None, :],
        0.0,
    )
    weight_hi, weight_lo = split_bf16(neg_weight + pos_weight)
    ctx_sum = jnp.einsum(
        "gpt,gtd->pd", weight_hi, query_blocks, preferred_element_type=jnp.float32
    ) + jnp.einsum("gpt,gtd->pd", weight_lo, query_blocks, preferred_element_type=jnp.float32)
    word_sum = spread_rows(word_sel, conj_product(query_grads, rel_used, half_width))
    slot_grad = slot_grad + 0.02 * live_mask[:, None] * own_table.astype(jnp.float32)
    outgoing = slot_grad.reshape(owner_count, slot_count, row_width)
    returned = lax.all_to_all(
        outgoing.astype(jnp.bfloat16), both, split_axis=0, concat_axis=0, tiled=True
    ).astype(outgoing.dtype)
    owner_map = (incoming.reshape(-1)[None, :] == jnp.arange(owned_rows)[:, None]).astype(
        jnp.float32
    )
    relation_grad = jnp.dot(
        owner_map,
        returned.reshape(-1, row_width),
        precision=lax.Precision.HIGHEST,
        preferred_element_type=jnp.float32,
    )
    return (word_sum.astype(jnp.bfloat16), ctx_sum.astype(jnp.bfloat16), relation_grad)


def solution(mesh):
    return jax.shard_map(
        shards,
        mesh=mesh,
        in_specs=(
            P("blk", None),
            P("blk", None),
            P(("blk", "rel"), None),
            P(("blk", "rel")),
            P(("blk", "rel")),
            P(("blk", "rel")),
            P(("blk", "rel"), None),
            P("blk", "rel", None, None, None),
            P("blk", "rel", None, None),
        ),
        out_specs=(P("blk", None), P("blk", None), P(("blk", "rel"), None)),
        check_vma=False,
    )
```

```python
import jax
import jax.numpy as jnp
from jax import lax
from jax.sharding import PartitionSpec as P
import functools
from jax.experimental import pallas as pl
from jax.experimental.pallas import tpu as pltpu


def passed_along(shard, axis, by):
    length = lax.axis_size(axis)
    return lax.ppermute(shard, axis, [(i, (i + by) % length) for i in range(length)])


def complex_product(left_vec, right_vec, half_width):
    left_re, left_im = (left_vec[..., :half_width], left_vec[..., half_width:])
    right_re, right_im = (right_vec[..., :half_width], right_vec[..., half_width:])
    return jnp.concatenate(
        [left_re * right_re - left_im * right_im, left_re * right_im + left_im * right_re], axis=-1
    )


def conj_product(grad_vec, other_vec, half_width):
    grad_re, grad_im = (grad_vec[..., :half_width], grad_vec[..., half_width:])
    other_re, other_im = (other_vec[..., :half_width], other_vec[..., half_width:])
    return jnp.concatenate(
        [grad_re * other_re + grad_im * other_im, grad_im * other_re - grad_re * other_im], axis=-1
    )


def one_hot(index_ids, row_total):
    return (index_ids[..., None] == jnp.arange(row_total)).astype(jnp.bfloat16)


def pick_rows(selector, rows):
    return jnp.dot(selector, rows, preferred_element_type=jnp.float32)


def split_bf16(values):
    upper = values.astype(jnp.bfloat16)
    lower = (values - upper.astype(jnp.float32)).astype(jnp.bfloat16)
    return upper, lower


def spread_rows(selector, terms):
    upper, lower = split_bf16(terms)
    dims = (((0,), (0,)), ((), ()))
    return lax.dot_general(
        selector, upper, dims, preferred_element_type=jnp.float32
    ) + lax.dot_general(selector, lower, dims, preferred_element_type=jnp.float32)


def _sigmoid(x):
    return 1.0 / (1.0 + jnp.exp(-x))


def _select(ids_col, total):
    hit = ids_col == lax.broadcasted_iota(jnp.int32, (ids_col.shape[0], total), 1)
    return jnp.where(hit, 1.0, 0.0).astype(jnp.bfloat16)


def _select_t(ids_row, total):
    hit = ids_row == lax.broadcasted_iota(jnp.int32, (total, ids_row.shape[1]), 0)
    return jnp.where(hit, 1.0, 0.0).astype(jnp.bfloat16)


def _mm(a, b):
    return jnp.dot(a, b, preferred_element_type=jnp.float32)


def _spread(sel_t, terms):
    upper = terms.astype(jnp.bfloat16)
    lower = (terms - upper.astype(jnp.float32)).astype(jnp.bfloat16)
    return _mm(sel_t, upper) + _mm(sel_t, lower)


def _chain_body(groups, own_groups, block, neg_count, scale,
                wcol, wrow, ccol, crow, scol, srow, ncol, nrow,
                words, held, table, word_out, ctx_out, slot_out):
    parts = words.shape[0]
    rows = table.shape[0]
    slots = slot_out.shape[0]
    half = words.shape[1] // 2
    word_out[...] = jnp.zeros(word_out.shape, jnp.float32)
    ctx_out[...] = jnp.zeros(ctx_out.shape, jnp.float32)
    slot_out[...] = jnp.zeros(slot_out.shape, jnp.float32)
    for g in range(groups):
        t0 = g * block
        w = _mm(_select(wcol[t0:t0 + block, :], parts), words[...])
        c = _mm(_select(ccol[t0:t0 + block, :], parts), held[...])
        rv = _mm(_select(scol[t0:t0 + block, :], rows), table[...])
        w_re, w_im = w[:, :half], w[:, half:]
        r_re, r_im = rv[:, :half], rv[:, half:]
        q = jnp.concatenate([w_re * r_re - w_im * r_im, w_re * r_im + w_im * r_re], axis=1)
        q = q.astype(jnp.bfloat16)
        qf = q.astype(jnp.float32)
        pos = jnp.sum(qf * c, axis=1, keepdims=True)
        dpos = -1.0 / (1.0 + jnp.exp(pos))
        n0 = g * neg_count
        neg_sel = _select(ncol[n0:n0 + neg_count, :], parts)
        neg = _mm(neg_sel, held[...]).astype(jnp.bfloat16)
        scores = lax.dot_general(q, neg, (((1,), (1,)), ((), ())),
                                 preferred_element_type=jnp.float32)
        dneg = (_sigmoid(scores) * scale).astype(jnp.bfloat16)
        gq = dpos * c + _mm(dneg, neg)
        g_re, g_im = gq[:, :half], gq[:, half:]
        if g < own_groups:
            rterm = jnp.concatenate([g_re * w_re + g_im * w_im, g_im * w_re - g_re * w_im], axis=1)
            slot_out[...] += _spread(_select_t(srow[:, t0:t0 + block], slots), rterm)
        wterm = jnp.concatenate([g_re * r_re + g_im * r_im, g_im * r_re - g_re * r_im], axis=1)
        word_out[...] += _spread(_select_t(wrow[:, t0:t0 + block], parts), wterm)
        ctx_t = _select_t(crow[:, t0:t0 + block], parts)
        neg_t = _select_t(nrow[g:g + 1, :], parts)
        neg_weight = lax.dot_general(neg_t, dneg, (((1,), (1,)), ((), ())),
                                     preferred_element_type=jnp.float32)
        ctx_out[...] += _spread(ctx_t, dpos * qf) + _spread(neg_weight, q)


def block_chains(word_ids, ctx_ids, slot_ids, neg_ids, own_groups, scale, words, held, table,
                 slots):
    trips = word_ids.shape[0]
    groups, neg_count = neg_ids.shape
    block = trips // groups
    parts, width = words.shape
    own_ids = slot_ids[: max(own_groups, 1) * block]
    body = functools.partial(_chain_body, groups, own_groups, block, neg_count, scale)
    return pl.pallas_call(
        body,
        out_shape=(
            jax.ShapeDtypeStruct((parts, width), jnp.float32),
            jax.ShapeDtypeStruct((parts, width), jnp.float32),
            jax.ShapeDtypeStruct((slots, width), jnp.float32),
        ),
        compiler_params=pltpu.CompilerParams(vmem_limit_bytes=48 * 1024 * 1024),
    )(
        word_ids.reshape(-1, 1),
        word_ids.reshape(1, -1),
        ctx_ids.reshape(-1, 1),
        ctx_ids.reshape(1, -1),
        slot_ids.reshape(-1, 1),
        own_ids.reshape(1, -1),
        neg_ids.reshape(-1, 1),
        neg_ids,
        words,
        held,
        table,
    )


def lanes_of(half_width):
    return -(-half_width // 128) * 128


def padded_halves(rows, half_width):
    count = rows.shape[0]
    lanes = lanes_of(half_width)
    return jnp.pad(
        rows.reshape(count, 2, half_width), ((0, 0), (0, 0), (0, lanes - half_width))
    ).reshape(count, 2 * lanes)


def unpadded_halves(rows, half_width):
    count = rows.shape[0]
    return rows.reshape(count, 2, lanes_of(half_width))[:, :, :half_width].reshape(
        count, 2 * half_width
    )


def shards(
    words, contexts, relations, word_index, context_index, rel_slot, neg_index, requests, counts
):
    row_width = words.shape[1]
    half_width = row_width // 2
    part_count = lax.axis_size("blk")
    split_count = lax.axis_size("rel")
    owner_count = part_count * split_count
    slot_count = requests.shape[-1]
    slot_total = owner_count * slot_count
    owned_rows = relations.shape[0]
    part_rows = contexts.shape[0]
    trips = word_index.shape[0]
    block_count = neg_index.shape[0]
    neg_count = neg_index.shape[1]
    block_size = trips // block_count
    neg_scale = float(neg_count) ** (-0.5)
    both = ("blk", "rel")

    held_rows = passed_along(contexts, "blk", 1)

    own_ints = jnp.concatenate([word_index, context_index, rel_slot, neg_index.reshape(-1)])
    bucket_ints = jnp.stack(
        [own_ints] + [passed_along(own_ints, "rel", -j) for j in range(1, split_count)]
    )
    word_ids = bucket_ints[:, :trips].reshape(-1)
    ctx_ids = bucket_ints[:, trips : 2 * trips].reshape(-1)
    slot_ids = (
        bucket_ints[:, 2 * trips : 3 * trips] + (jnp.arange(split_count) * slot_total)[:, None]
    ).reshape(-1)
    neg_ids = bucket_ints[:, 3 * trips :].reshape(split_count * block_count, neg_count)

    wanted = requests[0, 0].reshape(owner_count, slot_count)
    incoming = lax.all_to_all(wanted, both, split_axis=0, concat_axis=0, tiled=True)
    lists = incoming.reshape(part_count, split_count, slot_count)
    served = jnp.stack([jnp.roll(lists, -j, axis=1) for j in range(split_count)], axis=2)
    picked = pick_rows(one_hot(served.reshape(-1), owned_rows), relations).astype(
        jnp.bfloat16
    ).reshape(owner_count, split_count * slot_count, row_width)
    fetched = lax.all_to_all(picked, both, split_axis=0, concat_axis=0, tiled=True)
    live_mask = (
        (jnp.arange(slot_count)[None, :] < counts[0, 0].reshape(owner_count)[:, None])
        .reshape(-1)
        .astype(jnp.float32)
    )

    group_count = split_count * block_count
    word_table = padded_halves(words, half_width)
    held_table = padded_halves(held_rows, half_width)
    fetched, word_table, held_table = lax.optimization_barrier((fetched, word_table, held_table))
    slot_table = (
        fetched.reshape(owner_count, split_count, slot_count, row_width)
        .transpose(1, 0, 2, 3)
        .reshape(split_count * slot_total, row_width)
    )
    own_table = slot_table[:slot_total]
    rel_table = padded_halves(slot_table, half_width)
    own_word, own_ctx, own_slot = block_chains(
        word_ids[:trips], ctx_ids[:trips], slot_ids[:trips], neg_ids[:block_count],
        block_count, neg_scale, word_table, held_table, rel_table, slot_total,
    )
    rest_word, rest_ctx, _ = block_chains(
        word_ids[trips:], ctx_ids[trips:], slot_ids[trips:], neg_ids[block_count:],
        0, neg_scale, word_table, held_table, rel_table, 8,
    )
    word_sum = unpadded_halves(own_word + rest_word, half_width)
    ctx_sum = unpadded_halves(own_ctx + rest_ctx, half_width)
    slot_grad = unpadded_halves(own_slot, half_width)
    slot_grad = slot_grad + 0.02 * live_mask[:, None] * own_table.astype(jnp.float32)
    outgoing = slot_grad.reshape(owner_count, slot_count, row_width)
    returned = lax.all_to_all(
        outgoing.astype(jnp.bfloat16), both, split_axis=0, concat_axis=0, tiled=True
    ).astype(outgoing.dtype)
    owner_map = (incoming.reshape(-1)[None, :] == jnp.arange(owned_rows)[:, None]).astype(
        jnp.float32
    )
    relation_grad = jnp.dot(
        owner_map,
        returned.reshape(-1, row_width),
        precision=lax.Precision.HIGHEST,
        preferred_element_type=jnp.float32,
    )
    return (word_sum.astype(jnp.bfloat16), ctx_sum.astype(jnp.bfloat16), relation_grad)


def solution(mesh):
    return jax.shard_map(
        shards,
        mesh=mesh,
        in_specs=(
            P("blk", None),
            P("blk", None),
            P(("blk", "rel"), None),
            P(("blk", "rel")),
            P(("blk", "rel")),
            P(("blk", "rel")),
            P(("blk", "rel"), None),
            P("blk", "rel", None, None, None),
            P("blk", "rel", None, None),
        ),
        out_specs=(P("blk", None), P("blk", None), P(("blk", "rel"), None)),
        check_vma=False,
    )
```

```python
import jax
import jax.numpy as jnp
from jax import lax
from jax.sharding import PartitionSpec as P
import functools
from jax.experimental import pallas as pl
from jax.experimental.pallas import tpu as pltpu


def passed_along(shard, axis, by):
    length = lax.axis_size(axis)
    return lax.ppermute(shard, axis, [(i, (i + by) % length) for i in range(length)])


def complex_product(left_vec, right_vec, half_width):
    left_re, left_im = (left_vec[..., :half_width], left_vec[..., half_width:])
    right_re, right_im = (right_vec[..., :half_width], right_vec[..., half_width:])
    return jnp.concatenate(
        [left_re * right_re - left_im * right_im, left_re * right_im + left_im * right_re], axis=-1
    )


def conj_product(grad_vec, other_vec, half_width):
    grad_re, grad_im = (grad_vec[..., :half_width], grad_vec[..., half_width:])
    other_re, other_im = (other_vec[..., :half_width], other_vec[..., half_width:])
    return jnp.concatenate(
        [grad_re * other_re + grad_im * other_im, grad_im * other_re - grad_re * other_im], axis=-1
    )


def one_hot(index_ids, row_total):
    return (index_ids[..., None] == jnp.arange(row_total)).astype(jnp.bfloat16)


def pick_rows(selector, rows):
    return jnp.dot(selector, rows, preferred_element_type=jnp.float32)


def split_bf16(values):
    upper = values.astype(jnp.bfloat16)
    lower = (values - upper.astype(jnp.float32)).astype(jnp.bfloat16)
    return upper, lower


def spread_rows(selector, terms):
    upper, lower = split_bf16(terms)
    dims = (((0,), (0,)), ((), ()))
    return lax.dot_general(
        selector, upper, dims, preferred_element_type=jnp.float32
    ) + lax.dot_general(selector, lower, dims, preferred_element_type=jnp.float32)


def _sigmoid(x):
    return 1.0 / (1.0 + jnp.exp(-x))


def _select(ids_col, total):
    hit = ids_col == lax.broadcasted_iota(jnp.int32, (ids_col.shape[0], total), 1)
    return jnp.where(hit, 1.0, 0.0).astype(jnp.bfloat16)


def _select_t(ids_row, total):
    hit = ids_row == lax.broadcasted_iota(jnp.int32, (total, ids_row.shape[1]), 0)
    return jnp.where(hit, 1.0, 0.0).astype(jnp.bfloat16)


def _mm(a, b):
    return jnp.dot(a, b, preferred_element_type=jnp.float32)


def _spread(sel_t, terms):
    upper = terms.astype(jnp.bfloat16)
    lower = (terms - upper.astype(jnp.float32)).astype(jnp.bfloat16)
    return _mm(sel_t, upper) + _mm(sel_t, lower)


def _chain_body(groups, own_groups, block, neg_count, scale,
                wcol, wrow, ccol, crow, scol, srow, ncol, nrow, ocol, live,
                words, held, table, word_out, ctx_out, slot_out):
    parts = words.shape[0]
    rows = table.shape[0]
    slots = slot_out.shape[0]
    half = words.shape[1] // 2
    word_out[...] = jnp.zeros(word_out.shape, jnp.float32)
    ctx_out[...] = jnp.zeros(ctx_out.shape, jnp.float32)
    slot_sum = jnp.zeros(slot_out.shape, jnp.float32)
    for g in range(groups):
        t0 = g * block
        w = _mm(_select(wcol[t0:t0 + block, :], parts), words[...])
        c = _mm(_select(ccol[t0:t0 + block, :], parts), held[...])
        rv = _mm(_select(scol[t0:t0 + block, :], rows), table[...])
        w_re, w_im = w[:, :half], w[:, half:]
        r_re, r_im = rv[:, :half], rv[:, half:]
        q = jnp.concatenate([w_re * r_re - w_im * r_im, w_re * r_im + w_im * r_re], axis=1)
        q = q.astype(jnp.bfloat16)
        qf = q.astype(jnp.float32)
        pos = jnp.sum(qf * c, axis=1, keepdims=True)
        dpos = -1.0 / (1.0 + jnp.exp(pos))
        n0 = g * neg_count
        neg_sel = _select(ncol[n0:n0 + neg_count, :], parts)
        neg = _mm(neg_sel, held[...]).astype(jnp.bfloat16)
        scores = lax.dot_general(q, neg, (((1,), (1,)), ((), ())),
                                 preferred_element_type=jnp.float32)
        dneg = (_sigmoid(scores) * scale).astype(jnp.bfloat16)
        gq = dpos * c + _mm(dneg, neg)
        g_re, g_im = gq[:, :half], gq[:, half:]
        if g < own_groups:
            rterm = jnp.concatenate([g_re * w_re + g_im * w_im, g_im * w_re - g_re * w_im], axis=1)
            slot_sum = slot_sum + _spread(_select_t(srow[:, t0:t0 + block], slots), rterm)
        wterm = jnp.concatenate([g_re * r_re + g_im * r_im, g_im * r_re - g_re * r_im], axis=1)
        word_out[...] += _spread(_select_t(wrow[:, t0:t0 + block], parts), wterm)
        ctx_t = _select_t(crow[:, t0:t0 + block], parts)
        neg_t = _select_t(nrow[g:g + 1, :], parts)
        neg_weight = lax.dot_general(neg_t, dneg, (((1,), (1,)), ((), ())),
                                     preferred_element_type=jnp.float32)
        ctx_out[...] += _spread(ctx_t, dpos * qf) + _spread(neg_weight, q)
    if own_groups:
        own_rows = _mm(_select(ocol[...], rows), table[...])
        slot_sum = slot_sum + 0.02 * live[...] * own_rows
    slot_out[...] = slot_sum.astype(slot_out.dtype)


def block_chains(word_ids, ctx_ids, slot_ids, own_ids, neg_ids, own_groups, scale, words, held,
                 table, own_rows, live_mask):
    trips = word_ids.shape[0]
    groups, neg_count = neg_ids.shape
    block = trips // groups
    parts, width = words.shape
    body = functools.partial(_chain_body, groups, own_groups, block, neg_count, scale)
    return pl.pallas_call(
        body,
        out_shape=(
            jax.ShapeDtypeStruct((parts, width), jnp.float32),
            jax.ShapeDtypeStruct((parts, width), jnp.float32),
            jax.ShapeDtypeStruct((own_rows.shape[0], width), jnp.bfloat16),
        ),
        compiler_params=pltpu.CompilerParams(vmem_limit_bytes=48 * 1024 * 1024),
    )(
        word_ids.reshape(-1, 1),
        word_ids.reshape(1, -1),
        ctx_ids.reshape(-1, 1),
        ctx_ids.reshape(1, -1),
        slot_ids.reshape(-1, 1),
        own_ids.reshape(1, -1),
        neg_ids.reshape(-1, 1),
        neg_ids,
        own_rows.reshape(-1, 1),
        live_mask.reshape(-1, 1),
        words,
        held,
        table,
    )


def lanes_of(half_width):
    return -(-half_width // 128) * 128


def padded_halves(rows, half_width):
    count = rows.shape[0]
    lanes = lanes_of(half_width)
    return jnp.pad(
        rows.reshape(count, 2, half_width), ((0, 0), (0, 0), (0, lanes - half_width))
    ).reshape(count, 2 * lanes)


def unpadded_halves(rows, half_width):
    count = rows.shape[0]
    return rows.reshape(count, 2, lanes_of(half_width))[:, :, :half_width].reshape(
        count, 2 * half_width
    )


def shards(
    words, contexts, relations, word_index, context_index, rel_slot, neg_index, requests, counts
):
    row_width = words.shape[1]
    half_width = row_width // 2
    part_count = lax.axis_size("blk")
    split_count = lax.axis_size("rel")
    owner_count = part_count * split_count
    slot_count = requests.shape[-1]
    slot_total = owner_count * slot_count
    owned_rows = relations.shape[0]
    part_rows = contexts.shape[0]
    trips = word_index.shape[0]
    block_count = neg_index.shape[0]
    neg_count = neg_index.shape[1]
    block_size = trips // block_count
    neg_scale = float(neg_count) ** (-0.5)
    both = ("blk", "rel")

    held_rows = passed_along(contexts, "blk", 1)

    own_ints = jnp.concatenate([word_index, context_index, rel_slot, neg_index.reshape(-1)])
    bucket_ints = jnp.stack(
        [own_ints] + [passed_along(own_ints, "rel", -j) for j in range(1, split_count)]
    )
    word_ids = bucket_ints[:, :trips].reshape(-1)
    ctx_ids = bucket_ints[:, trips : 2 * trips].reshape(-1)
    slot_ids = bucket_ints[:, 2 * trips : 3 * trips]
    slot_ids = (
        (slot_ids // slot_count) * (split_count * slot_count)
        + (jnp.arange(split_count) * slot_count)[:, None]
        + slot_ids % slot_count
    ).reshape(-1)
    own_slots = jnp.arange(slot_total)
    own_rows = (own_slots // slot_count) * (split_count * slot_count) + own_slots % slot_count
    neg_ids = bucket_ints[:, 3 * trips :].reshape(split_count * block_count, neg_count)

    wanted = requests[0, 0].reshape(owner_count, slot_count)
    incoming = lax.all_to_all(wanted, both, split_axis=0, concat_axis=0, tiled=True)
    lists = incoming.reshape(part_count, split_count, slot_count)
    served = jnp.stack([jnp.roll(lists, -j, axis=1) for j in range(split_count)], axis=2)
    padded_width = 2 * lanes_of(half_width)
    picked = pick_rows(
        one_hot(served.reshape(-1), owned_rows), padded_halves(relations, half_width)
    ).astype(jnp.bfloat16).reshape(owner_count, split_count * slot_count, padded_width)
    fetched = lax.all_to_all(picked, both, split_axis=0, concat_axis=0, tiled=True)
    live_mask = (
        (jnp.arange(slot_count)[None, :] < counts[0, 0].reshape(owner_count)[:, None])
        .reshape(-1)
        .astype(jnp.float32)
    )

    group_count = split_count * block_count
    word_table = padded_halves(words, half_width)
    held_table = padded_halves(held_rows, half_width)
    fetched, word_table, held_table = lax.optimization_barrier((fetched, word_table, held_table))
    rel_table = fetched.reshape(split_count * slot_total, padded_width)
    own_word, own_ctx, own_slot = block_chains(
        word_ids[:trips], ctx_ids[:trips], slot_ids[:trips], rel_slot, neg_ids[:block_count],
        block_count, neg_scale, word_table, held_table, rel_table, own_rows, live_mask,
    )
    rest_word, rest_ctx, _ = block_chains(
        word_ids[trips:], ctx_ids[trips:], slot_ids[trips:], rel_slot, neg_ids[block_count:],
        0, neg_scale, word_table, held_table, rel_table, own_rows[:8], live_mask[:8],
    )
    word_sum = unpadded_halves(own_word + rest_word, half_width)
    ctx_sum = unpadded_halves(own_ctx + rest_ctx, half_width)
    returned = lax.all_to_all(
        own_slot.reshape(owner_count, slot_count, padded_width),
        both,
        split_axis=0,
        concat_axis=0,
        tiled=True,
    ).astype(jnp.float32)
    owner_map = (incoming.reshape(-1)[None, :] == jnp.arange(owned_rows)[:, None]).astype(
        jnp.float32
    )
    relation_grad = jnp.dot(
        owner_map,
        returned.reshape(-1, padded_width),
        precision=lax.Precision.HIGHEST,
        preferred_element_type=jnp.float32,
    )
    relation_grad = unpadded_halves(relation_grad, half_width)
    return (word_sum.astype(jnp.bfloat16), ctx_sum.astype(jnp.bfloat16), relation_grad)


def solution(mesh):
    return jax.shard_map(
        shards,
        mesh=mesh,
        in_specs=(
            P("blk", None),
            P("blk", None),
            P(("blk", "rel"), None),
            P(("blk", "rel")),
            P(("blk", "rel")),
            P(("blk", "rel")),
            P(("blk", "rel"), None),
            P("blk", "rel", None, None, None),
            P("blk", "rel", None, None),
        ),
        out_specs=(P("blk", None), P("blk", None), P(("blk", "rel"), None)),
        check_vma=False,
    )
```

```python
import jax
import jax.numpy as jnp
from jax import lax
from jax.sharding import PartitionSpec as P
import functools
from jax.experimental import pallas as pl
from jax.experimental.pallas import tpu as pltpu


def passed_along(shard, axis, by):
    length = lax.axis_size(axis)
    return lax.ppermute(shard, axis, [(i, (i + by) % length) for i in range(length)])


def complex_product(left_vec, right_vec, half_width):
    left_re, left_im = (left_vec[..., :half_width], left_vec[..., half_width:])
    right_re, right_im = (right_vec[..., :half_width], right_vec[..., half_width:])
    return jnp.concatenate(
        [left_re * right_re - left_im * right_im, left_re * right_im + left_im * right_re], axis=-1
    )


def conj_product(grad_vec, other_vec, half_width):
    grad_re, grad_im = (grad_vec[..., :half_width], grad_vec[..., half_width:])
    other_re, other_im = (other_vec[..., :half_width], other_vec[..., half_width:])
    return jnp.concatenate(
        [grad_re * other_re + grad_im * other_im, grad_im * other_re - grad_re * other_im], axis=-1
    )


def one_hot(index_ids, row_total):
    return (index_ids[..., None] == jnp.arange(row_total)).astype(jnp.bfloat16)


def pick_rows(selector, rows):
    return jnp.dot(selector, rows, preferred_element_type=jnp.float32)


def split_bf16(values):
    upper = values.astype(jnp.bfloat16)
    lower = (values - upper.astype(jnp.float32)).astype(jnp.bfloat16)
    return upper, lower


def spread_rows(selector, terms):
    upper, lower = split_bf16(terms)
    dims = (((0,), (0,)), ((), ()))
    return lax.dot_general(
        selector, upper, dims, preferred_element_type=jnp.float32
    ) + lax.dot_general(selector, lower, dims, preferred_element_type=jnp.float32)


def _sigmoid(x):
    return 1.0 / (1.0 + jnp.exp(-x))


def _select_t(ids_row, total):
    hit = ids_row == lax.broadcasted_iota(jnp.int32, (total, ids_row.shape[1]), 0)
    return jnp.where(hit, 1.0, 0.0).astype(jnp.bfloat16)


def _mm(a, b):
    return jnp.dot(a, b, preferred_element_type=jnp.float32)


def _pick(sel_t, rows):
    return lax.dot_general(sel_t, rows, (((0,), (0,)), ((), ())),
                           preferred_element_type=jnp.float32)


def _spread(sel_t, terms):
    upper = terms.astype(jnp.bfloat16)
    lower = (terms - upper.astype(jnp.float32)).astype(jnp.bfloat16)
    return _mm(sel_t, upper) + _mm(sel_t, lower)


def _chain_body(groups, own_groups, block, neg_count, scale,
                wrow, crow, scomb, srow, nrow, orow, live,
                words, held, table, word_out, ctx_out, slot_out):
    parts = words.shape[0]
    rows = table.shape[0]
    slots = slot_out.shape[0]
    half = words.shape[1] // 2
    word_out[...] = jnp.zeros(word_out.shape, jnp.float32)
    ctx_out[...] = jnp.zeros(ctx_out.shape, jnp.float32)
    slot_sum = jnp.zeros(slot_out.shape, jnp.float32)
    for g in range(groups):
        t0 = g * block
        word_t = _select_t(wrow[:, t0:t0 + block], parts)
        ctx_t = _select_t(crow[:, t0:t0 + block], parts)
        w = _pick(word_t, words[...])
        c = _pick(ctx_t, held[...])
        rv = _pick(_select_t(scomb[:, t0:t0 + block], rows), table[...])
        w_re, w_im = w[:, :half], w[:, half:]
        r_re, r_im = rv[:, :half], rv[:, half:]
        q = jnp.concatenate([w_re * r_re - w_im * r_im, w_re * r_im + w_im * r_re], axis=1)
        q = q.astype(jnp.bfloat16)
        qf = q.astype(jnp.float32)
        pos = jnp.sum(qf * c, axis=1, keepdims=True)
        dpos = -1.0 / (1.0 + jnp.exp(pos))
        neg_t = _select_t(nrow[g:g + 1, :], parts)
        neg = _pick(neg_t, held[...]).astype(jnp.bfloat16)
        scores = lax.dot_general(q, neg, (((1,), (1,)), ((), ())),
                                 preferred_element_type=jnp.float32)
        dneg = (_sigmoid(scores) * scale).astype(jnp.bfloat16)
        gq = dpos * c + _mm(dneg, neg)
        g_re, g_im = gq[:, :half], gq[:, half:]
        if g < own_groups:
            rterm = jnp.concatenate([g_re * w_re + g_im * w_im, g_im * w_re - g_re * w_im], axis=1)
            slot_sum = slot_sum + _spread(_select_t(srow[:, t0:t0 + block], slots), rterm)
        wterm = jnp.concatenate([g_re * r_re + g_im * r_im, g_im * r_re - g_re * r_im], axis=1)
        word_out[...] += _spread(word_t, wterm)
        neg_weight = lax.dot_general(neg_t, dneg, (((1,), (1,)), ((), ())),
                                     preferred_element_type=jnp.float32)
        ctx_out[...] += _spread(ctx_t, dpos * qf) + _spread(neg_weight, q)
    if own_groups:
        hit = orow[...] == lax.broadcasted_iota(jnp.int32, (rows, orow.shape[1]), 0)
        live_t = jnp.where(hit, live[...], 0.0).astype(jnp.bfloat16)
        slot_sum = slot_sum + 0.02 * _pick(live_t, table[...])
    slot_out[...] = slot_sum.astype(slot_out.dtype)


def block_chains(word_ids, ctx_ids, slot_ids, own_ids, neg_ids, own_groups, scale, words, held,
                 table, own_rows, live_mask):
    trips = word_ids.shape[0]
    groups, neg_count = neg_ids.shape
    block = trips // groups
    parts, width = words.shape
    body = functools.partial(_chain_body, groups, own_groups, block, neg_count, scale)
    return pl.pallas_call(
        body,
        out_shape=(
            jax.ShapeDtypeStruct((parts, width), jnp.float32),
            jax.ShapeDtypeStruct((parts, width), jnp.float32),
            jax.ShapeDtypeStruct((own_rows.shape[0], width), jnp.bfloat16),
        ),
        compiler_params=pltpu.CompilerParams(vmem_limit_bytes=48 * 1024 * 1024),
    )(
        word_ids.reshape(1, -1),
        ctx_ids.reshape(1, -1),
        slot_ids.reshape(1, -1),
        own_ids.reshape(1, -1),
        neg_ids,
        own_rows.reshape(1, -1),
        live_mask.reshape(1, -1),
        words,
        held,
        table,
    )


def lanes_of(half_width):
    return -(-half_width // 128) * 128


def padded_halves(rows, half_width):
    count = rows.shape[0]
    lanes = lanes_of(half_width)
    return jnp.pad(
        rows.reshape(count, 2, half_width), ((0, 0), (0, 0), (0, lanes - half_width))
    ).reshape(count, 2 * lanes)


def unpadded_halves(rows, half_width):
    count = rows.shape[0]
    return rows.reshape(count, 2, lanes_of(half_width))[:, :, :half_width].reshape(
        count, 2 * half_width
    )


def shards(
    words, contexts, relations, word_index, context_index, rel_slot, neg_index, requests, counts
):
    row_width = words.shape[1]
    half_width = row_width // 2
    part_count = lax.axis_size("blk")
    split_count = lax.axis_size("rel")
    owner_count = part_count * split_count
    slot_count = requests.shape[-1]
    slot_total = owner_count * slot_count
    owned_rows = relations.shape[0]
    part_rows = contexts.shape[0]
    trips = word_index.shape[0]
    block_count = neg_index.shape[0]
    neg_count = neg_index.shape[1]
    block_size = trips // block_count
    neg_scale = float(neg_count) ** (-0.5)
    both = ("blk", "rel")

    held_rows = passed_along(contexts, "blk", 1)

    own_ints = jnp.concatenate([word_index, context_index, rel_slot, neg_index.reshape(-1)])
    bucket_ints = jnp.stack(
        [own_ints] + [passed_along(own_ints, "rel", -j) for j in range(1, split_count)]
    )
    word_ids = bucket_ints[:, :trips].reshape(-1)
    ctx_ids = bucket_ints[:, trips : 2 * trips].reshape(-1)
    slot_ids = bucket_ints[:, 2 * trips : 3 * trips]
    slot_ids = (
        (slot_ids // slot_count) * (split_count * slot_count)
        + (jnp.arange(split_count) * slot_count)[:, None]
        + slot_ids % slot_count
    ).reshape(-1)
    own_slots = jnp.arange(slot_total)
    own_rows = (own_slots // slot_count) * (split_count * slot_count) + own_slots % slot_count
    neg_ids = bucket_ints[:, 3 * trips :].reshape(split_count * block_count, neg_count)

    wanted = requests[0, 0].reshape(owner_count, slot_count)
    incoming = lax.all_to_all(wanted, both, split_axis=0, concat_axis=0, tiled=True)
    lists = incoming.reshape(part_count, split_count, slot_count)
    served = jnp.stack([jnp.roll(lists, -j, axis=1) for j in range(split_count)], axis=2)
    padded_width = 2 * lanes_of(half_width)
    picked = pick_rows(
        one_hot(served.reshape(-1), owned_rows), padded_halves(relations, half_width)
    ).astype(jnp.bfloat16).reshape(owner_count, split_count * slot_count, padded_width)
    fetched = lax.all_to_all(picked, both, split_axis=0, concat_axis=0, tiled=True)
    live_mask = (
        (jnp.arange(slot_count)[None, :] < counts[0, 0].reshape(owner_count)[:, None])
        .reshape(-1)
        .astype(jnp.float32)
    )

    group_count = split_count * block_count
    word_table = padded_halves(words, half_width)
    held_table = padded_halves(held_rows, half_width)
    fetched, word_table, held_table = lax.optimization_barrier((fetched, word_table, held_table))
    rel_table = fetched.reshape(split_count * slot_total, padded_width)
    own_word, own_ctx, own_slot = block_chains(
        word_ids[:trips], ctx_ids[:trips], slot_ids[:trips], rel_slot, neg_ids[:block_count],
        block_count, neg_scale, word_table, held_table, rel_table, own_rows, live_mask,
    )
    rest_word, rest_ctx, _ = block_chains(
        word_ids[trips:], ctx_ids[trips:], slot_ids[trips:], rel_slot, neg_ids[block_count:],
        0, neg_scale, word_table, held_table, rel_table, own_rows[:8], live_mask[:8],
    )
    word_sum = unpadded_halves(own_word + rest_word, half_width)
    ctx_sum = unpadded_halves(own_ctx + rest_ctx, half_width)
    returned = lax.all_to_all(
        own_slot.reshape(owner_count, slot_count, padded_width),
        both,
        split_axis=0,
        concat_axis=0,
        tiled=True,
    ).astype(jnp.float32)
    owner_map = (incoming.reshape(-1)[None, :] == jnp.arange(owned_rows)[:, None]).astype(
        jnp.float32
    )
    relation_grad = jnp.dot(
        owner_map,
        returned.reshape(-1, padded_width),
        precision=lax.Precision.HIGHEST,
        preferred_element_type=jnp.float32,
    )
    relation_grad = unpadded_halves(relation_grad, half_width)
    return (word_sum.astype(jnp.bfloat16), ctx_sum.astype(jnp.bfloat16), relation_grad)


def solution(mesh):
    return jax.shard_map(
        shards,
        mesh=mesh,
        in_specs=(
            P("blk", None),
            P("blk", None),
            P(("blk", "rel"), None),
            P(("blk", "rel")),
            P(("blk", "rel")),
            P(("blk", "rel")),
            P(("blk", "rel"), None),
            P("blk", "rel", None, None, None),
            P("blk", "rel", None, None),
        ),
        out_specs=(P("blk", None), P("blk", None), P(("blk", "rel"), None)),
        check_vma=False,
    )
```

```python
import jax
import jax.numpy as jnp
from jax import lax
from jax.sharding import PartitionSpec as P
import functools
from jax.experimental import pallas as pl
from jax.experimental.pallas import tpu as pltpu


def passed_along(shard, axis, by):
    length = lax.axis_size(axis)
    return lax.ppermute(shard, axis, [(i, (i + by) % length) for i in range(length)])


def complex_product(left_vec, right_vec, half_width):
    left_re, left_im = (left_vec[..., :half_width], left_vec[..., half_width:])
    right_re, right_im = (right_vec[..., :half_width], right_vec[..., half_width:])
    return jnp.concatenate(
        [left_re * right_re - left_im * right_im, left_re * right_im + left_im * right_re], axis=-1
    )


def conj_product(grad_vec, other_vec, half_width):
    grad_re, grad_im = (grad_vec[..., :half_width], grad_vec[..., half_width:])
    other_re, other_im = (other_vec[..., :half_width], other_vec[..., half_width:])
    return jnp.concatenate(
        [grad_re * other_re + grad_im * other_im, grad_im * other_re - grad_re * other_im], axis=-1
    )


def one_hot(index_ids, row_total):
    return (index_ids[..., None] == jnp.arange(row_total)).astype(jnp.bfloat16)


def pick_rows(selector, rows):
    return jnp.dot(selector, rows, preferred_element_type=jnp.float32)


def split_bf16(values):
    upper = values.astype(jnp.bfloat16)
    lower = (values - upper.astype(jnp.float32)).astype(jnp.bfloat16)
    return upper, lower


def spread_rows(selector, terms):
    upper, lower = split_bf16(terms)
    dims = (((0,), (0,)), ((), ()))
    return lax.dot_general(
        selector, upper, dims, preferred_element_type=jnp.float32
    ) + lax.dot_general(selector, lower, dims, preferred_element_type=jnp.float32)


def _sigmoid(x):
    return 1.0 / (1.0 + jnp.exp(-x))


def _select_t(ids_row, total):
    hit = ids_row == lax.broadcasted_iota(jnp.int32, (total, ids_row.shape[1]), 0)
    return jnp.where(hit, 1.0, 0.0).astype(jnp.bfloat16)


def _mm(a, b):
    return jnp.dot(a, b, preferred_element_type=jnp.float32)


def _pick(sel_t, rows):
    return lax.dot_general(sel_t, rows, (((0,), (0,)), ((), ())),
                           preferred_element_type=jnp.float32)


def _spread(sel_t, terms):
    upper = terms.astype(jnp.bfloat16)
    lower = (terms - upper.astype(jnp.float32)).astype(jnp.bfloat16)
    return _mm(sel_t, upper) + _mm(sel_t, lower)


def _chain_body(groups, own_groups, block, neg_count, scale,
                wrow, crow, scomb, srow, nrow, orow, live,
                words, held, table, word_out, ctx_out, slot_out):
    parts = words.shape[0]
    rows = table.shape[0]
    slots = slot_out.shape[0]
    half = words.shape[1] // 2
    word_out[...] = jnp.zeros(word_out.shape, jnp.float32)
    ctx_out[...] = jnp.zeros(ctx_out.shape, jnp.float32)
    slot_sum = jnp.zeros(slot_out.shape, jnp.float32)
    for g in range(groups):
        t0 = g * block
        word_t = _select_t(wrow[:, t0:t0 + block], parts)
        ctx_t = _select_t(crow[:, t0:t0 + block], parts)
        w = _pick(word_t, words[...])
        c = _pick(ctx_t, held[...])
        rv = _pick(_select_t(scomb[:, t0:t0 + block], rows), table[...])
        w_re, w_im = w[:, :half], w[:, half:]
        r_re, r_im = rv[:, :half], rv[:, half:]
        q = jnp.concatenate([w_re * r_re - w_im * r_im, w_re * r_im + w_im * r_re], axis=1)
        q = q.astype(jnp.bfloat16)
        qf = q.astype(jnp.float32)
        pos = jnp.sum(qf * c, axis=1, keepdims=True)
        dpos = -1.0 / (1.0 + jnp.exp(pos))
        neg_t = _select_t(nrow[g:g + 1, :], parts)
        neg = _pick(neg_t, held[...]).astype(jnp.bfloat16)
        scores = lax.dot_general(q, neg, (((1,), (1,)), ((), ())),
                                 preferred_element_type=jnp.float32)
        dneg = (_sigmoid(scores) * scale).astype(jnp.bfloat16)
        gq = dpos * c + _mm(dneg, neg)
        g_re, g_im = gq[:, :half], gq[:, half:]
        if g < own_groups:
            rterm = jnp.concatenate([g_re * w_re + g_im * w_im, g_im * w_re - g_re * w_im], axis=1)
            slot_sum = slot_sum + _spread(_select_t(srow[:, t0:t0 + block], slots), rterm)
        wterm = jnp.concatenate([g_re * r_re + g_im * r_im, g_im * r_re - g_re * r_im], axis=1)
        word_out[...] += _spread(word_t, wterm)
        neg_weight = lax.dot_general(neg_t, dneg, (((1,), (1,)), ((), ())),
                                     preferred_element_type=jnp.float32)
        ctx_out[...] += _spread(ctx_t, dpos * qf) + _spread(neg_weight, q)
    if own_groups:
        hit = orow[...] == lax.broadcasted_iota(jnp.int32, (rows, orow.shape[1]), 0)
        live_t = jnp.where(hit, live[...], 0.0).astype(jnp.bfloat16)
        slot_sum = slot_sum + 0.02 * _pick(live_t, table[...])
    slot_out[...] = slot_sum.astype(slot_out.dtype)


def block_chains(word_ids, ctx_ids, slot_ids, own_ids, neg_ids, own_groups, scale, words, held,
                 table, own_rows, live_mask):
    trips = word_ids.shape[0]
    groups, neg_count = neg_ids.shape
    block = trips // groups
    parts, width = words.shape
    body = functools.partial(_chain_body, groups, own_groups, block, neg_count, scale)
    return pl.pallas_call(
        body,
        out_shape=(
            jax.ShapeDtypeStruct((parts, width), jnp.float32),
            jax.ShapeDtypeStruct((parts, width), jnp.float32),
            jax.ShapeDtypeStruct((own_rows.shape[0], width), jnp.bfloat16),
        ),
        compiler_params=pltpu.CompilerParams(vmem_limit_bytes=48 * 1024 * 1024),
    )(
        word_ids.reshape(1, -1),
        ctx_ids.reshape(1, -1),
        slot_ids.reshape(1, -1),
        own_ids.reshape(1, -1),
        neg_ids,
        own_rows.reshape(1, -1),
        live_mask.reshape(1, -1),
        words,
        held,
        table,
    )


def lanes_of(half_width):
    return -(-half_width // 128) * 128


def padded_halves(rows, half_width):
    count = rows.shape[0]
    lanes = lanes_of(half_width)
    return jnp.pad(
        rows.reshape(count, 2, half_width), ((0, 0), (0, 0), (0, lanes - half_width))
    ).reshape(count, 2 * lanes)


def unpadded_halves(rows, half_width):
    count = rows.shape[0]
    return rows.reshape(count, 2, lanes_of(half_width))[:, :, :half_width].reshape(
        count, 2 * half_width
    )


def shards(
    words, contexts, relations, word_index, context_index, rel_slot, neg_index, requests, counts
):
    row_width = words.shape[1]
    half_width = row_width // 2
    part_count = lax.axis_size("blk")
    split_count = lax.axis_size("rel")
    owner_count = part_count * split_count
    slot_count = requests.shape[-1]
    slot_total = owner_count * slot_count
    owned_rows = relations.shape[0]
    part_rows = contexts.shape[0]
    trips = word_index.shape[0]
    block_count = neg_index.shape[0]
    neg_count = neg_index.shape[1]
    block_size = trips // block_count
    neg_scale = float(neg_count) ** (-0.5)
    both = ("blk", "rel")

    held_rows = passed_along(contexts, "blk", 1)

    own_ints = jnp.concatenate([word_index, context_index, rel_slot, neg_index.reshape(-1)])
    bucket_ints = jnp.stack(
        [own_ints] + [passed_along(own_ints, "rel", -j) for j in range(1, split_count)]
    )
    word_ids = bucket_ints[:, :trips].reshape(-1)
    ctx_ids = bucket_ints[:, trips : 2 * trips].reshape(-1)
    slot_ids = bucket_ints[:, 2 * trips : 3 * trips]
    slot_ids = (
        (slot_ids // slot_count) * (split_count * slot_count)
        + (jnp.arange(split_count) * slot_count)[:, None]
        + slot_ids % slot_count
    ).reshape(-1)
    own_slots = jnp.arange(slot_total)
    own_rows = (own_slots // slot_count) * (split_count * slot_count) + own_slots % slot_count
    neg_ids = bucket_ints[:, 3 * trips :].reshape(split_count * block_count, neg_count)

    wanted = requests[0, 0].reshape(owner_count, slot_count)
    incoming = lax.all_to_all(wanted, both, split_axis=0, concat_axis=0, tiled=True)
    lists = incoming.reshape(part_count, split_count, slot_count)
    served = jnp.stack([jnp.roll(lists, -j, axis=1) for j in range(split_count)], axis=2)
    padded_width = 2 * lanes_of(half_width)
    picked = pick_rows(one_hot(served.reshape(-1), owned_rows), relations).astype(
        jnp.bfloat16
    ).reshape(owner_count, split_count * slot_count, row_width)
    fetched = lax.all_to_all(picked, both, split_axis=0, concat_axis=0, tiled=True)
    live_mask = (
        (jnp.arange(slot_count)[None, :] < counts[0, 0].reshape(owner_count)[:, None])
        .reshape(-1)
        .astype(jnp.float32)
    )

    group_count = split_count * block_count
    word_table = padded_halves(words, half_width)
    held_table = padded_halves(held_rows, half_width)
    fetched, word_table, held_table = lax.optimization_barrier((fetched, word_table, held_table))
    rel_table = padded_halves(fetched.reshape(split_count * slot_total, row_width), half_width)
    own_word, own_ctx, own_slot = block_chains(
        word_ids[:trips], ctx_ids[:trips], slot_ids[:trips], rel_slot, neg_ids[:block_count],
        block_count, neg_scale, word_table, held_table, rel_table, own_rows, live_mask,
    )
    rest_word, rest_ctx, _ = block_chains(
        word_ids[trips:], ctx_ids[trips:], slot_ids[trips:], rel_slot, neg_ids[block_count:],
        0, neg_scale, word_table, held_table, rel_table, own_rows[:8], live_mask[:8],
    )
    word_sum = unpadded_halves(own_word + rest_word, half_width)
    ctx_sum = unpadded_halves(own_ctx + rest_ctx, half_width)
    returned = lax.all_to_all(
        own_slot.reshape(owner_count, slot_count, padded_width),
        both,
        split_axis=0,
        concat_axis=0,
        tiled=True,
    ).astype(jnp.float32)
    owner_map = (incoming.reshape(-1)[None, :] == jnp.arange(owned_rows)[:, None]).astype(
        jnp.float32
    )
    relation_grad = jnp.dot(
        owner_map,
        returned.reshape(-1, padded_width),
        precision=lax.Precision.HIGHEST,
        preferred_element_type=jnp.float32,
    )
    relation_grad = unpadded_halves(relation_grad, half_width)
    return (word_sum.astype(jnp.bfloat16), ctx_sum.astype(jnp.bfloat16), relation_grad)


def solution(mesh):
    return jax.shard_map(
        shards,
        mesh=mesh,
        in_specs=(
            P("blk", None),
            P("blk", None),
            P(("blk", "rel"), None),
            P(("blk", "rel")),
            P(("blk", "rel")),
            P(("blk", "rel")),
            P(("blk", "rel"), None),
            P("blk", "rel", None, None, None),
            P("blk", "rel", None, None),
        ),
        out_specs=(P("blk", None), P("blk", None), P(("blk", "rel"), None)),
        check_vma=False,
    )
```

```python
import jax
import jax.numpy as jnp
from jax import lax
from jax.sharding import PartitionSpec as P
import functools
from jax.experimental import pallas as pl
from jax.experimental.pallas import tpu as pltpu


def passed_along(shard, axis, by):
    length = lax.axis_size(axis)
    return lax.ppermute(shard, axis, [(i, (i + by) % length) for i in range(length)])


def complex_product(left_vec, right_vec, half_width):
    left_re, left_im = (left_vec[..., :half_width], left_vec[..., half_width:])
    right_re, right_im = (right_vec[..., :half_width], right_vec[..., half_width:])
    return jnp.concatenate(
        [left_re * right_re - left_im * right_im, left_re * right_im + left_im * right_re], axis=-1
    )


def conj_product(grad_vec, other_vec, half_width):
    grad_re, grad_im = (grad_vec[..., :half_width], grad_vec[..., half_width:])
    other_re, other_im = (other_vec[..., :half_width], other_vec[..., half_width:])
    return jnp.concatenate(
        [grad_re * other_re + grad_im * other_im, grad_im * other_re - grad_re * other_im], axis=-1
    )


def one_hot(index_ids, row_total):
    return (index_ids[..., None] == jnp.arange(row_total)).astype(jnp.bfloat16)


def pick_rows(selector, rows):
    return jnp.dot(selector, rows, preferred_element_type=jnp.float32)


def split_bf16(values):
    upper = values.astype(jnp.bfloat16)
    lower = (values - upper.astype(jnp.float32)).astype(jnp.bfloat16)
    return upper, lower


def spread_rows(selector, terms):
    upper, lower = split_bf16(terms)
    dims = (((0,), (0,)), ((), ()))
    return lax.dot_general(
        selector, upper, dims, preferred_element_type=jnp.float32
    ) + lax.dot_general(selector, lower, dims, preferred_element_type=jnp.float32)


def _sigmoid(x):
    return 1.0 / (1.0 + jnp.exp(-x))


def _select_t(ids_row, total):
    hit = ids_row == lax.broadcasted_iota(jnp.int32, (total, ids_row.shape[1]), 0)
    return jnp.where(hit, 1.0, 0.0).astype(jnp.bfloat16)


def _mm(a, b):
    return jnp.dot(a, b, preferred_element_type=jnp.float32)


def _pick(sel_t, rows):
    return lax.dot_general(sel_t, rows, (((0,), (0,)), ((), ())),
                           preferred_element_type=jnp.float32)


def _spread(sel_t, terms):
    upper = terms.astype(jnp.bfloat16)
    lower = (terms - upper.astype(jnp.float32)).astype(jnp.bfloat16)
    return _mm(sel_t, upper) + _mm(sel_t, lower)


def _chain_body(groups, own_groups, block, neg_count, scale,
                wrow, crow, scomb, srow, nrow, live,
                words, held, table, word_out, ctx_out, slot_out):
    parts = words.shape[0]
    rows = table.shape[0]
    half = words.shape[1] // 2
    word_out[...] = jnp.zeros(word_out.shape, jnp.float32)
    ctx_out[...] = jnp.zeros(ctx_out.shape, jnp.float32)
    slot_sum = jnp.zeros(slot_out.shape, jnp.float32)
    rterms = []
    for g in range(groups):
        t0 = g * block
        word_t = _select_t(wrow[:, t0:t0 + block], parts)
        ctx_t = _select_t(crow[:, t0:t0 + block], parts)
        w = _pick(word_t, words[...])
        c = _pick(ctx_t, held[...])
        rv = _pick(_select_t(scomb[:, t0:t0 + block], rows), table[...])
        w_re, w_im = w[:, :half], w[:, half:]
        r_re, r_im = rv[:, :half], rv[:, half:]
        q = jnp.concatenate([w_re * r_re - w_im * r_im, w_re * r_im + w_im * r_re], axis=1)
        q = q.astype(jnp.bfloat16)
        qf = q.astype(jnp.float32)
        pos = jnp.sum(qf * c, axis=1, keepdims=True)
        dpos = -1.0 / (1.0 + jnp.exp(pos))
        neg_t = _select_t(nrow[g:g + 1, :], parts)
        neg = _pick(neg_t, held[...]).astype(jnp.bfloat16)
        scores = lax.dot_general(q, neg, (((1,), (1,)), ((), ())),
                                 preferred_element_type=jnp.float32)
        dneg = (_sigmoid(scores) * scale).astype(jnp.bfloat16)
        gq = dpos * c + _mm(dneg, neg)
        g_re, g_im = gq[:, :half], gq[:, half:]
        if g < own_groups:
            rterm = jnp.concatenate([g_re * w_re + g_im * w_im, g_im * w_re - g_re * w_im], axis=1)
            rterms.append(rterm)
        wterm = jnp.concatenate([g_re * r_re + g_im * r_im, g_im * r_re - g_re * r_im], axis=1)
        word_out[...] += _spread(word_t, wterm)
        neg_weight = lax.dot_general(neg_t, dneg, (((1,), (1,)), ((), ())),
                                     preferred_element_type=jnp.float32)
        ctx_out[...] += _spread(ctx_t, dpos * qf) + _spread(neg_weight, q)
    if own_groups:
        entries = live.shape[0]
        owners = slot_out.shape[0]
        pieces = []
        for entry in range(entries):
            piece = jnp.zeros((owners, words.shape[1]), jnp.float32)
            for g in range(own_groups):
                t0 = g * block
                ids = srow[:, t0:t0 + block]
                hit = ids == lax.broadcasted_iota(jnp.int32, (owners, block), 0) * entries + entry
                sel_t = jnp.where(hit, 1.0, 0.0).astype(jnp.bfloat16)
                piece = piece + _spread(sel_t, rterms[g])
            own = lax.broadcasted_iota(jnp.int32, (rows, owners), 1) * (rows // owners) + entry
            own_hit = own == lax.broadcasted_iota(jnp.int32, (rows, owners), 0)
            own_sel_t = jnp.where(own_hit, live[entry:entry + 1, :], 0.0).astype(jnp.bfloat16)
            piece = piece + 0.02 * _pick(own_sel_t, table[...])
            pieces.append(piece)
        slot_sum = jnp.concatenate(pieces, axis=1)
    slot_out[...] = slot_sum.astype(slot_out.dtype)


def block_chains(word_ids, ctx_ids, slot_ids, own_ids, neg_ids, own_groups, scale, words, held,
                 table, live_mask):
    trips = word_ids.shape[0]
    groups, neg_count = neg_ids.shape
    block = trips // groups
    parts, width = words.shape
    body = functools.partial(_chain_body, groups, own_groups, block, neg_count, scale)
    return pl.pallas_call(
        body,
        out_shape=(
            jax.ShapeDtypeStruct((parts, width), jnp.float32),
            jax.ShapeDtypeStruct((parts, width), jnp.float32),
            jax.ShapeDtypeStruct((live_mask.shape[1], live_mask.shape[0] * width), jnp.bfloat16),
        ),
        compiler_params=pltpu.CompilerParams(vmem_limit_bytes=48 * 1024 * 1024),
    )(
        word_ids.reshape(1, -1),
        ctx_ids.reshape(1, -1),
        slot_ids.reshape(1, -1),
        own_ids.reshape(1, -1),
        neg_ids,
        live_mask,
        words,
        held,
        table,
    )


def lanes_of(half_width):
    return -(-half_width // 128) * 128


def padded_halves(rows, half_width):
    count = rows.shape[0]
    lanes = lanes_of(half_width)
    return jnp.pad(
        rows.reshape(count, 2, half_width), ((0, 0), (0, 0), (0, lanes - half_width))
    ).reshape(count, 2 * lanes)


def unpadded_halves(rows, half_width):
    count = rows.shape[0]
    return rows.reshape(count, 2, lanes_of(half_width))[:, :, :half_width].reshape(
        count, 2 * half_width
    )


def shards(
    words, contexts, relations, word_index, context_index, rel_slot, neg_index, requests, counts
):
    row_width = words.shape[1]
    half_width = row_width // 2
    part_count = lax.axis_size("blk")
    split_count = lax.axis_size("rel")
    owner_count = part_count * split_count
    slot_count = requests.shape[-1]
    slot_total = owner_count * slot_count
    owned_rows = relations.shape[0]
    part_rows = contexts.shape[0]
    trips = word_index.shape[0]
    block_count = neg_index.shape[0]
    neg_count = neg_index.shape[1]
    block_size = trips // block_count
    neg_scale = float(neg_count) ** (-0.5)
    both = ("blk", "rel")

    held_rows = passed_along(contexts, "blk", 1)

    own_ints = jnp.concatenate([word_index, context_index, rel_slot, neg_index.reshape(-1)])
    bucket_ints = jnp.stack(
        [own_ints] + [passed_along(own_ints, "rel", -j) for j in range(1, split_count)]
    )
    word_ids = bucket_ints[:, :trips].reshape(-1)
    ctx_ids = bucket_ints[:, trips : 2 * trips].reshape(-1)
    slot_ids = bucket_ints[:, 2 * trips : 3 * trips]
    slot_ids = (
        (slot_ids // slot_count) * (split_count * slot_count)
        + (jnp.arange(split_count) * slot_count)[:, None]
        + slot_ids % slot_count
    ).reshape(-1)
    neg_ids = bucket_ints[:, 3 * trips :].reshape(split_count * block_count, neg_count)

    wanted = requests[0, 0].reshape(owner_count, slot_count)
    incoming = lax.all_to_all(wanted, both, split_axis=0, concat_axis=0, tiled=True)
    lists = incoming.reshape(part_count, split_count, slot_count)
    served = jnp.stack([jnp.roll(lists, -j, axis=1) for j in range(split_count)], axis=2)
    padded_width = 2 * lanes_of(half_width)
    picked = pick_rows(one_hot(served.reshape(-1), owned_rows), relations).astype(
        jnp.bfloat16
    ).reshape(owner_count, split_count * slot_count, row_width)
    fetched = lax.all_to_all(picked, both, split_axis=0, concat_axis=0, tiled=True)
    live_mask = (
        (jnp.arange(slot_count)[None, :] < counts[0, 0].reshape(owner_count)[:, None])
        .reshape(-1)
        .astype(jnp.float32)
    )

    group_count = split_count * block_count
    live_rows = live_mask.reshape(owner_count, slot_count).T
    word_table = padded_halves(words, half_width)
    held_table = padded_halves(held_rows, half_width)
    fetched, word_table, held_table = lax.optimization_barrier((fetched, word_table, held_table))
    rel_table = padded_halves(fetched.reshape(split_count * slot_total, row_width), half_width)
    own_word, own_ctx, own_slot = block_chains(
        word_ids[:trips], ctx_ids[:trips], slot_ids[:trips], rel_slot, neg_ids[:block_count],
        block_count, neg_scale, word_table, held_table, rel_table, live_rows,
    )
    rest_word, rest_ctx, _ = block_chains(
        word_ids[trips:], ctx_ids[trips:], slot_ids[trips:], rel_slot, neg_ids[block_count:],
        0, neg_scale, word_table, held_table, rel_table, live_rows[:, :8],
    )
    word_sum = unpadded_halves(own_word + rest_word, half_width)
    ctx_sum = unpadded_halves(own_ctx + rest_ctx, half_width)
    returned = lax.all_to_all(own_slot, both, split_axis=0, concat_axis=0, tiled=True)
    requested = incoming.reshape(owner_count, slot_count)
    relation_grad = sum(
        jnp.dot(
            (requested[:, entry][None, :] == jnp.arange(owned_rows)[:, None]).astype(jnp.float32),
            returned[:, entry * padded_width : (entry + 1) * padded_width].astype(jnp.float32),
            precision=lax.Precision.HIGHEST,
            preferred_element_type=jnp.float32,
        )
        for entry in range(slot_count)
    )
    relation_grad = unpadded_halves(relation_grad, half_width)
    return (word_sum.astype(jnp.bfloat16), ctx_sum.astype(jnp.bfloat16), relation_grad)


def solution(mesh):
    return jax.shard_map(
        shards,
        mesh=mesh,
        in_specs=(
            P("blk", None),
            P("blk", None),
            P(("blk", "rel"), None),
            P(("blk", "rel")),
            P(("blk", "rel")),
            P(("blk", "rel")),
            P(("blk", "rel"), None),
            P("blk", "rel", None, None, None),
            P("blk", "rel", None, None),
        ),
        out_specs=(P("blk", None), P("blk", None), P(("blk", "rel"), None)),
        check_vma=False,
    )
```

```python
import jax
import jax.numpy as jnp
from jax import lax
from jax.sharding import PartitionSpec as P
import functools
from jax.experimental import pallas as pl
from jax.experimental.pallas import tpu as pltpu


def passed_along(shard, axis, by):
    length = lax.axis_size(axis)
    return lax.ppermute(shard, axis, [(i, (i + by) % length) for i in range(length)])


def complex_product(left_vec, right_vec, half_width):
    left_re, left_im = (left_vec[..., :half_width], left_vec[..., half_width:])
    right_re, right_im = (right_vec[..., :half_width], right_vec[..., half_width:])
    return jnp.concatenate(
        [left_re * right_re - left_im * right_im, left_re * right_im + left_im * right_re], axis=-1
    )


def conj_product(grad_vec, other_vec, half_width):
    grad_re, grad_im = (grad_vec[..., :half_width], grad_vec[..., half_width:])
    other_re, other_im = (other_vec[..., :half_width], other_vec[..., half_width:])
    return jnp.concatenate(
        [grad_re * other_re + grad_im * other_im, grad_im * other_re - grad_re * other_im], axis=-1
    )


def one_hot(index_ids, row_total):
    return (index_ids[..., None] == jnp.arange(row_total)).astype(jnp.bfloat16)


def pick_rows(selector, rows):
    return jnp.dot(selector, rows, preferred_element_type=jnp.float32)


def split_bf16(values):
    upper = values.astype(jnp.bfloat16)
    lower = (values - upper.astype(jnp.float32)).astype(jnp.bfloat16)
    return upper, lower


def spread_rows(selector, terms):
    upper, lower = split_bf16(terms)
    dims = (((0,), (0,)), ((), ()))
    return lax.dot_general(
        selector, upper, dims, preferred_element_type=jnp.float32
    ) + lax.dot_general(selector, lower, dims, preferred_element_type=jnp.float32)


def _sigmoid(x):
    return 1.0 / (1.0 + jnp.exp(-x))


def _select_t(ids_row, total):
    hit = ids_row == lax.broadcasted_iota(jnp.int32, (total, ids_row.shape[1]), 0)
    return jnp.where(hit, 1.0, 0.0).astype(jnp.bfloat16)


def _mm(a, b):
    return jnp.dot(a, b, preferred_element_type=jnp.float32)


def _pick(sel_t, rows):
    return lax.dot_general(sel_t, rows, (((0,), (0,)), ((), ())),
                           preferred_element_type=jnp.float32)


def _spread(sel_t, terms):
    upper = terms.astype(jnp.bfloat16)
    lower = (terms - upper.astype(jnp.float32)).astype(jnp.bfloat16)
    return _mm(sel_t, upper) + _mm(sel_t, lower)


def _chain_body(groups, own_groups, block, neg_count, scale,
                wrow, crow, scomb, srow, nrow, orow, live,
                words, held, table, word_out, ctx_out, slot_out):
    parts = words.shape[0]
    rows = table.shape[0]
    slots = slot_out.shape[0]
    half = words.shape[1] // 2
    word_out[...] = jnp.zeros(word_out.shape, jnp.float32)
    ctx_out[...] = jnp.zeros(ctx_out.shape, jnp.float32)
    slot_sum = jnp.zeros((slot_out.shape[0], words.shape[1]), jnp.float32)
    for g in range(groups):
        t0 = g * block
        word_t = _select_t(wrow[:, t0:t0 + block], parts)
        ctx_t = _select_t(crow[:, t0:t0 + block], parts)
        w = _pick(word_t, words[...])
        c = _pick(ctx_t, held[...])
        rv = _pick(_select_t(scomb[:, t0:t0 + block], rows), table[...])
        w_re, w_im = w[:, :half], w[:, half:]
        r_re, r_im = rv[:, :half], rv[:, half:]
        q = jnp.concatenate([w_re * r_re - w_im * r_im, w_re * r_im + w_im * r_re], axis=1)
        q = q.astype(jnp.bfloat16)
        qf = q.astype(jnp.float32)
        pos = jnp.sum(qf * c, axis=1, keepdims=True)
        dpos = -1.0 / (1.0 + jnp.exp(pos))
        neg_t = _select_t(nrow[g:g + 1, :], parts)
        neg = _pick(neg_t, held[...]).astype(jnp.bfloat16)
        scores = lax.dot_general(q, neg, (((1,), (1,)), ((), ())),
                                 preferred_element_type=jnp.float32)
        dneg = (_sigmoid(scores) * scale).astype(jnp.bfloat16)
        gq = dpos * c + _mm(dneg, neg)
        g_re, g_im = gq[:, :half], gq[:, half:]
        if g < own_groups:
            rterm = jnp.concatenate([g_re * w_re + g_im * w_im, g_im * w_re - g_re * w_im], axis=1)
            slot_sum = slot_sum + _spread(_select_t(srow[:, t0:t0 + block], slots), rterm)
        wterm = jnp.concatenate([g_re * r_re + g_im * r_im, g_im * r_re - g_re * r_im], axis=1)
        word_out[...] += _spread(word_t, wterm)
        neg_weight = lax.dot_general(neg_t, dneg, (((1,), (1,)), ((), ())),
                                     preferred_element_type=jnp.float32)
        ctx_out[...] += _spread(ctx_t, dpos * qf) + _spread(neg_weight, q)
    if own_groups:
        hit = orow[...] == lax.broadcasted_iota(jnp.int32, (rows, orow.shape[1]), 0)
        live_t = jnp.where(hit, live[...], 0.0).astype(jnp.bfloat16)
        slot_sum = slot_sum + 0.02 * _pick(live_t, table[...])
    kept = slot_out.shape[1] // 2
    slot_out[:, :kept] = slot_sum[:, :kept].astype(slot_out.dtype)
    slot_out[:, kept:] = slot_sum[:, half:half + kept].astype(slot_out.dtype)


def block_chains(word_ids, ctx_ids, slot_ids, own_ids, neg_ids, own_groups, scale, words, held,
                 table, own_rows, live_mask, row_width):
    trips = word_ids.shape[0]
    groups, neg_count = neg_ids.shape
    block = trips // groups
    parts, width = words.shape
    body = functools.partial(_chain_body, groups, own_groups, block, neg_count, scale)
    return pl.pallas_call(
        body,
        out_shape=(
            jax.ShapeDtypeStruct((parts, width), jnp.float32),
            jax.ShapeDtypeStruct((parts, width), jnp.float32),
            jax.ShapeDtypeStruct((own_rows.shape[0], row_width), jnp.bfloat16),
        ),
        compiler_params=pltpu.CompilerParams(vmem_limit_bytes=48 * 1024 * 1024),
    )(
        word_ids.reshape(1, -1),
        ctx_ids.reshape(1, -1),
        slot_ids.reshape(1, -1),
        own_ids.reshape(1, -1),
        neg_ids,
        own_rows.reshape(1, -1),
        live_mask.reshape(1, -1),
        words,
        held,
        table,
    )


def lanes_of(half_width):
    return -(-half_width // 128) * 128


def padded_halves(rows, half_width):
    count = rows.shape[0]
    lanes = lanes_of(half_width)
    return jnp.pad(
        rows.reshape(count, 2, half_width), ((0, 0), (0, 0), (0, lanes - half_width))
    ).reshape(count, 2 * lanes)


def unpadded_halves(rows, half_width):
    count = rows.shape[0]
    return rows.reshape(count, 2, lanes_of(half_width))[:, :, :half_width].reshape(
        count, 2 * half_width
    )


def shards(
    words, contexts, relations, word_index, context_index, rel_slot, neg_index, requests, counts
):
    row_width = words.shape[1]
    half_width = row_width // 2
    part_count = lax.axis_size("blk")
    split_count = lax.axis_size("rel")
    owner_count = part_count * split_count
    slot_count = requests.shape[-1]
    slot_total = owner_count * slot_count
    owned_rows = relations.shape[0]
    part_rows = contexts.shape[0]
    trips = word_index.shape[0]
    block_count = neg_index.shape[0]
    neg_count = neg_index.shape[1]
    block_size = trips // block_count
    neg_scale = float(neg_count) ** (-0.5)
    both = ("blk", "rel")

    held_rows = passed_along(contexts, "blk", 1)

    own_ints = jnp.concatenate([word_index, context_index, rel_slot, neg_index.reshape(-1)])
    bucket_ints = jnp.stack(
        [own_ints] + [passed_along(own_ints, "rel", -j) for j in range(1, split_count)]
    )
    word_ids = bucket_ints[:, :trips].reshape(-1)
    ctx_ids = bucket_ints[:, trips : 2 * trips].reshape(-1)
    slot_ids = bucket_ints[:, 2 * trips : 3 * trips]
    slot_ids = (
        (slot_ids // slot_count) * (split_count * slot_count)
        + (jnp.arange(split_count) * slot_count)[:, None]
        + slot_ids % slot_count
    ).reshape(-1)
    own_slots = jnp.arange(slot_total)
    own_rows = (own_slots // slot_count) * (split_count * slot_count) + own_slots % slot_count
    neg_ids = bucket_ints[:, 3 * trips :].reshape(split_count * block_count, neg_count)

    wanted = requests[0, 0].reshape(owner_count, slot_count)
    incoming = lax.all_to_all(wanted, both, split_axis=0, concat_axis=0, tiled=True)
    lists = incoming.reshape(part_count, split_count, slot_count)
    served = jnp.stack([jnp.roll(lists, -j, axis=1) for j in range(split_count)], axis=2)
    padded_width = 2 * lanes_of(half_width)
    picked = pick_rows(one_hot(served.reshape(-1), owned_rows), relations).astype(
        jnp.bfloat16
    ).reshape(owner_count, split_count * slot_count, row_width)
    fetched = lax.all_to_all(picked, both, split_axis=0, concat_axis=0, tiled=True)
    live_mask = (
        (jnp.arange(slot_count)[None, :] < counts[0, 0].reshape(owner_count)[:, None])
        .reshape(-1)
        .astype(jnp.float32)
    )

    group_count = split_count * block_count
    word_table = padded_halves(words, half_width)
    held_table = padded_halves(held_rows, half_width)
    fetched, word_table, held_table = lax.optimization_barrier((fetched, word_table, held_table))
    rel_table = padded_halves(fetched.reshape(split_count * slot_total, row_width), half_width)
    own_word, own_ctx, own_slot = block_chains(
        word_ids[:trips], ctx_ids[:trips], slot_ids[:trips], rel_slot, neg_ids[:block_count],
        block_count, neg_scale, word_table, held_table, rel_table, own_rows, live_mask,
        row_width,
    )
    rest_word, rest_ctx, _ = block_chains(
        word_ids[trips:], ctx_ids[trips:], slot_ids[trips:], rel_slot, neg_ids[block_count:],
        0, neg_scale, word_table, held_table, rel_table, own_rows[:8], live_mask[:8],
        row_width,
    )
    word_sum = unpadded_halves(own_word + rest_word, half_width)
    ctx_sum = unpadded_halves(own_ctx + rest_ctx, half_width)
    returned = lax.all_to_all(
        own_slot.reshape(owner_count, slot_count, row_width),
        both,
        split_axis=0,
        concat_axis=0,
        tiled=True,
    ).astype(jnp.float32)
    owner_map = (incoming.reshape(-1)[None, :] == jnp.arange(owned_rows)[:, None]).astype(
        jnp.float32
    )
    relation_grad = jnp.dot(
        owner_map,
        returned.reshape(-1, row_width),
        precision=lax.Precision.HIGHEST,
        preferred_element_type=jnp.float32,
    )
    return (word_sum.astype(jnp.bfloat16), ctx_sum.astype(jnp.bfloat16), relation_grad)


def solution(mesh):
    return jax.shard_map(
        shards,
        mesh=mesh,
        in_specs=(
            P("blk", None),
            P("blk", None),
            P(("blk", "rel"), None),
            P(("blk", "rel")),
            P(("blk", "rel")),
            P(("blk", "rel")),
            P(("blk", "rel"), None),
            P("blk", "rel", None, None, None),
            P("blk", "rel", None, None),
        ),
        out_specs=(P("blk", None), P("blk", None), P(("blk", "rel"), None)),
        check_vma=False,
    )
```

```python
import jax
import jax.numpy as jnp
from jax import lax
from jax.sharding import PartitionSpec as P
import functools
from jax.experimental import pallas as pl
from jax.experimental.pallas import tpu as pltpu


def passed_along(shard, axis, by):
    length = lax.axis_size(axis)
    return lax.ppermute(shard, axis, [(i, (i + by) % length) for i in range(length)])


def complex_product(left_vec, right_vec, half_width):
    left_re, left_im = (left_vec[..., :half_width], left_vec[..., half_width:])
    right_re, right_im = (right_vec[..., :half_width], right_vec[..., half_width:])
    return jnp.concatenate(
        [left_re * right_re - left_im * right_im, left_re * right_im + left_im * right_re], axis=-1
    )


def conj_product(grad_vec, other_vec, half_width):
    grad_re, grad_im = (grad_vec[..., :half_width], grad_vec[..., half_width:])
    other_re, other_im = (other_vec[..., :half_width], other_vec[..., half_width:])
    return jnp.concatenate(
        [grad_re * other_re + grad_im * other_im, grad_im * other_re - grad_re * other_im], axis=-1
    )


def one_hot(index_ids, row_total):
    return (index_ids[..., None] == jnp.arange(row_total)).astype(jnp.bfloat16)


def pick_rows(selector, rows):
    return jnp.dot(selector, rows, preferred_element_type=jnp.float32)


def split_bf16(values):
    upper = values.astype(jnp.bfloat16)
    lower = (values - upper.astype(jnp.float32)).astype(jnp.bfloat16)
    return upper, lower


def spread_rows(selector, terms):
    upper, lower = split_bf16(terms)
    dims = (((0,), (0,)), ((), ()))
    return lax.dot_general(
        selector, upper, dims, preferred_element_type=jnp.float32
    ) + lax.dot_general(selector, lower, dims, preferred_element_type=jnp.float32)


def _sigmoid(x):
    return 1.0 / (1.0 + jnp.exp(-x))


def _select_t(ids_row, total):
    hit = ids_row == lax.broadcasted_iota(jnp.int32, (total, ids_row.shape[1]), 0)
    return jnp.where(hit, 1.0, 0.0).astype(jnp.bfloat16)


def _mm(a, b):
    return jnp.dot(a, b, preferred_element_type=jnp.float32)


def _pick(sel_t, rows):
    return lax.dot_general(sel_t, rows, (((0,), (0,)), ((), ())),
                           preferred_element_type=jnp.float32)


def _spread(sel_t, terms):
    upper = terms.astype(jnp.bfloat16)
    lower = (terms - upper.astype(jnp.float32)).astype(jnp.bfloat16)
    return _mm(sel_t, upper) + _mm(sel_t, lower)


def _chain_body(groups, own_groups, block, neg_count, scale,
                wrow, crow, scomb, srow, nrow, orow, live,
                words, held, table, word_out, ctx_out, slot_out):
    parts = words.shape[0]
    rows = table.shape[0]
    slots = slot_out.shape[0]
    half = words.shape[1] // 2
    word_out[...] = jnp.zeros(word_out.shape, jnp.float32)
    ctx_out[...] = jnp.zeros(ctx_out.shape, jnp.float32)
    slot_sum = jnp.zeros((slot_out.shape[0], words.shape[1]), jnp.float32)
    for g in range(groups):
        t0 = g * block
        word_t = _select_t(wrow[:, t0:t0 + block], parts)
        ctx_t = _select_t(crow[:, t0:t0 + block], parts)
        w = _pick(word_t, words[...])
        c = _pick(ctx_t, held[...])
        rv = _pick(_select_t(scomb[:, t0:t0 + block], rows), table[...])
        w_re, w_im = w[:, :half], w[:, half:]
        r_re, r_im = rv[:, :half], rv[:, half:]
        q = jnp.concatenate([w_re * r_re - w_im * r_im, w_re * r_im + w_im * r_re], axis=1)
        q = q.astype(jnp.bfloat16)
        qf = q.astype(jnp.float32)
        pos = jnp.sum(qf * c, axis=1, keepdims=True)
        dpos = -1.0 / (1.0 + jnp.exp(pos))
        neg_t = _select_t(nrow[g:g + 1, :], parts)
        neg = _pick(neg_t, held[...]).astype(jnp.bfloat16)
        scores = lax.dot_general(q, neg, (((1,), (1,)), ((), ())),
                                 preferred_element_type=jnp.float32)
        dneg = (_sigmoid(scores) * scale).astype(jnp.bfloat16)
        gq = dpos * c + _mm(dneg, neg)
        g_re, g_im = gq[:, :half], gq[:, half:]
        if g < own_groups:
            rterm = jnp.concatenate([g_re * w_re + g_im * w_im, g_im * w_re - g_re * w_im], axis=1)
            slot_sum = slot_sum + _spread(_select_t(srow[:, t0:t0 + block], slots), rterm)
        wterm = jnp.concatenate([g_re * r_re + g_im * r_im, g_im * r_re - g_re * r_im], axis=1)
        word_out[...] += _spread(word_t, wterm)
        neg_weight = lax.dot_general(neg_t, dneg, (((1,), (1,)), ((), ())),
                                     preferred_element_type=jnp.float32)
        ctx_out[...] += _spread(ctx_t, dpos * qf) + _spread(neg_weight, q)
    if own_groups:
        hit = orow[...] == lax.broadcasted_iota(jnp.int32, (rows, orow.shape[1]), 0)
        live_t = jnp.where(hit, live[...], 0.0).astype(jnp.bfloat16)
        slot_sum = slot_sum + 0.02 * _pick(live_t, table[...])
    kept = slot_out.shape[1] // 2
    slot_out[:, :kept] = slot_sum[:, :kept].astype(slot_out.dtype)
    slot_out[:, kept:] = slot_sum[:, half:half + kept].astype(slot_out.dtype)


def block_chains(word_ids, ctx_ids, slot_ids, own_ids, neg_ids, own_groups, scale, words, held,
                 table, own_rows, live_mask, row_width):
    trips = word_ids.shape[0]
    groups, neg_count = neg_ids.shape
    block = trips // groups
    parts, width = words.shape
    body = functools.partial(_chain_body, groups, own_groups, block, neg_count, scale)
    return pl.pallas_call(
        body,
        out_shape=(
            jax.ShapeDtypeStruct((parts, width), jnp.float32),
            jax.ShapeDtypeStruct((parts, width), jnp.float32),
            jax.ShapeDtypeStruct((own_rows.shape[0], row_width), jnp.bfloat16),
        ),
        compiler_params=pltpu.CompilerParams(vmem_limit_bytes=48 * 1024 * 1024),
    )(
        word_ids.reshape(1, -1),
        ctx_ids.reshape(1, -1),
        slot_ids.reshape(1, -1),
        own_ids.reshape(1, -1),
        neg_ids,
        own_rows.reshape(1, -1),
        live_mask.reshape(1, -1),
        words,
        held,
        table,
    )


def lanes_of(half_width):
    return -(-half_width // 128) * 128


def padded_halves(rows, half_width):
    count = rows.shape[0]
    lanes = lanes_of(half_width)
    return jnp.pad(
        rows.reshape(count, 2, half_width), ((0, 0), (0, 0), (0, lanes - half_width))
    ).reshape(count, 2 * lanes)


def unpadded_halves(rows, half_width):
    count = rows.shape[0]
    return rows.reshape(count, 2, lanes_of(half_width))[:, :, :half_width].reshape(
        count, 2 * half_width
    )


def shards(
    words, contexts, relations, word_index, context_index, rel_slot, neg_index, requests, counts
):
    row_width = words.shape[1]
    half_width = row_width // 2
    part_count = lax.axis_size("blk")
    split_count = lax.axis_size("rel")
    owner_count = part_count * split_count
    slot_count = requests.shape[-1]
    slot_total = owner_count * slot_count
    owned_rows = relations.shape[0]
    part_rows = contexts.shape[0]
    trips = word_index.shape[0]
    block_count = neg_index.shape[0]
    neg_count = neg_index.shape[1]
    block_size = trips // block_count
    neg_scale = float(neg_count) ** (-0.5)
    both = ("blk", "rel")

    held_rows = passed_along(contexts, "blk", 1)

    own_ints = jnp.concatenate([word_index, context_index, rel_slot, neg_index.reshape(-1)])
    bucket_ints = jnp.stack(
        [own_ints] + [passed_along(own_ints, "rel", -j) for j in range(1, split_count)]
    )
    word_ids = bucket_ints[:, :trips].reshape(-1)
    ctx_ids = bucket_ints[:, trips : 2 * trips].reshape(-1)
    slot_ids = bucket_ints[:, 2 * trips : 3 * trips]
    slot_ids = (
        (slot_ids // slot_count) * (split_count * slot_count)
        + (jnp.arange(split_count) * slot_count)[:, None]
        + slot_ids % slot_count
    ).reshape(-1)
    own_slots = jnp.arange(slot_total)
    own_rows = (own_slots // slot_count) * (split_count * slot_count) + own_slots % slot_count
    neg_ids = bucket_ints[:, 3 * trips :].reshape(split_count * block_count, neg_count)

    wanted = requests[0, 0].reshape(owner_count, slot_count)
    incoming = lax.all_to_all(wanted, both, split_axis=0, concat_axis=0, tiled=True)
    lists = incoming.reshape(part_count, split_count, slot_count)
    served = jnp.stack([jnp.roll(lists, -j, axis=1) for j in range(split_count)], axis=2)
    padded_width = 2 * lanes_of(half_width)
    picked = jnp.einsum(
        "dkr,rf->dkf",
        one_hot(served.reshape(owner_count, split_count * slot_count), owned_rows),
        relations,
        preferred_element_type=jnp.float32,
    ).astype(jnp.bfloat16)
    fetched = lax.all_to_all(picked, both, split_axis=0, concat_axis=0, tiled=True)
    live_mask = (
        (jnp.arange(slot_count)[None, :] < counts[0, 0].reshape(owner_count)[:, None])
        .reshape(-1)
        .astype(jnp.float32)
    )

    group_count = split_count * block_count
    word_table = padded_halves(words, half_width)
    held_table = padded_halves(held_rows, half_width)
    fetched, word_table, held_table = lax.optimization_barrier((fetched, word_table, held_table))
    rel_table = padded_halves(fetched.reshape(split_count * slot_total, row_width), half_width)
    own_word, own_ctx, own_slot = block_chains(
        word_ids[:trips], ctx_ids[:trips], slot_ids[:trips], rel_slot, neg_ids[:block_count],
        block_count, neg_scale, word_table, held_table, rel_table, own_rows, live_mask,
        row_width,
    )
    rest_word, rest_ctx, _ = block_chains(
        word_ids[trips:], ctx_ids[trips:], slot_ids[trips:], rel_slot, neg_ids[block_count:],
        0, neg_scale, word_table, held_table, rel_table, own_rows[:8], live_mask[:8],
        row_width,
    )
    word_sum = unpadded_halves(own_word + rest_word, half_width)
    ctx_sum = unpadded_halves(own_ctx + rest_ctx, half_width)
    returned = lax.all_to_all(
        own_slot.reshape(owner_count, slot_count, row_width),
        both,
        split_axis=0,
        concat_axis=0,
        tiled=True,
    ).astype(jnp.float32)
    incoming, returned = lax.optimization_barrier((incoming, returned))
    owner_map = (incoming.reshape(-1)[None, :] == jnp.arange(owned_rows)[:, None]).astype(
        jnp.float32
    )
    relation_grad = jnp.dot(
        owner_map,
        returned.reshape(-1, row_width),
        precision=lax.Precision.HIGHEST,
        preferred_element_type=jnp.float32,
    )
    return (word_sum.astype(jnp.bfloat16), ctx_sum.astype(jnp.bfloat16), relation_grad)


def solution(mesh):
    return jax.shard_map(
        shards,
        mesh=mesh,
        in_specs=(
            P("blk", None),
            P("blk", None),
            P(("blk", "rel"), None),
            P(("blk", "rel")),
            P(("blk", "rel")),
            P(("blk", "rel")),
            P(("blk", "rel"), None),
            P("blk", "rel", None, None, None),
            P("blk", "rel", None, None),
        ),
        out_specs=(P("blk", None), P("blk", None), P(("blk", "rel"), None)),
        check_vma=False,
    )
```

```python
import jax
import jax.numpy as jnp
from jax import lax
from jax.sharding import PartitionSpec as P
import functools
from jax.experimental import pallas as pl
from jax.experimental.pallas import tpu as pltpu


def passed_along(shard, axis, by):
    length = lax.axis_size(axis)
    return lax.ppermute(shard, axis, [(i, (i + by) % length) for i in range(length)])


def complex_product(left_vec, right_vec, half_width):
    left_re, left_im = (left_vec[..., :half_width], left_vec[..., half_width:])
    right_re, right_im = (right_vec[..., :half_width], right_vec[..., half_width:])
    return jnp.concatenate(
        [left_re * right_re - left_im * right_im, left_re * right_im + left_im * right_re], axis=-1
    )


def conj_product(grad_vec, other_vec, half_width):
    grad_re, grad_im = (grad_vec[..., :half_width], grad_vec[..., half_width:])
    other_re, other_im = (other_vec[..., :half_width], other_vec[..., half_width:])
    return jnp.concatenate(
        [grad_re * other_re + grad_im * other_im, grad_im * other_re - grad_re * other_im], axis=-1
    )


def one_hot(index_ids, row_total):
    return (index_ids[..., None] == jnp.arange(row_total)).astype(jnp.bfloat16)


def pick_rows(selector, rows):
    return jnp.dot(selector, rows, preferred_element_type=jnp.float32)


def split_bf16(values):
    upper = values.astype(jnp.bfloat16)
    lower = (values - upper.astype(jnp.float32)).astype(jnp.bfloat16)
    return upper, lower


def spread_rows(selector, terms):
    upper, lower = split_bf16(terms)
    dims = (((0,), (0,)), ((), ()))
    return lax.dot_general(
        selector, upper, dims, preferred_element_type=jnp.float32
    ) + lax.dot_general(selector, lower, dims, preferred_element_type=jnp.float32)


def _sigmoid(x):
    return 1.0 / (1.0 + jnp.exp(-x))


def _select_t(ids_row, total):
    hit = ids_row == lax.broadcasted_iota(jnp.int32, (total, ids_row.shape[1]), 0)
    return jnp.where(hit, 1.0, 0.0).astype(jnp.bfloat16)


def _mm(a, b):
    return jnp.dot(a, b, preferred_element_type=jnp.float32)


def _pick(sel_t, rows):
    return lax.dot_general(sel_t, rows, (((0,), (0,)), ((), ())),
                           preferred_element_type=jnp.float32)


def _spread(sel_t, terms):
    upper = terms.astype(jnp.bfloat16)
    lower = (terms - upper.astype(jnp.float32)).astype(jnp.bfloat16)
    return _mm(sel_t, upper) + _mm(sel_t, lower)


def _chain_body(groups, own_groups, block, neg_count, scale,
                wrow, crow, scomb, srow, nrow, orow, live,
                words, held, table, word_out, ctx_out, slot_out):
    parts = words.shape[0]
    rows = table.shape[0]
    slots = slot_out.shape[0]
    half = words.shape[1] // 2
    word_out[...] = jnp.zeros(word_out.shape, jnp.float32)
    ctx_out[...] = jnp.zeros(ctx_out.shape, jnp.float32)
    slot_sum = jnp.zeros((slot_out.shape[0], words.shape[1]), jnp.float32)
    for g in range(groups):
        t0 = g * block
        word_t = _select_t(wrow[:, t0:t0 + block], parts)
        ctx_t = _select_t(crow[:, t0:t0 + block], parts)
        w = _pick(word_t, words[...])
        c = _pick(ctx_t, held[...])
        rv = _pick(_select_t(scomb[:, t0:t0 + block], rows), table[...])
        w_re, w_im = w[:, :half], w[:, half:]
        r_re, r_im = rv[:, :half], rv[:, half:]
        q = jnp.concatenate([w_re * r_re - w_im * r_im, w_re * r_im + w_im * r_re], axis=1)
        q = q.astype(jnp.bfloat16)
        qf = q.astype(jnp.float32)
        pos = jnp.sum(qf * c, axis=1, keepdims=True)
        dpos = -1.0 / (1.0 + jnp.exp(pos))
        neg_t = _select_t(nrow[g:g + 1, :], parts)
        neg = _pick(neg_t, held[...]).astype(jnp.bfloat16)
        scores = lax.dot_general(q, neg, (((1,), (1,)), ((), ())),
                                 preferred_element_type=jnp.float32)
        dneg = (_sigmoid(scores) * scale).astype(jnp.bfloat16)
        gq = dpos * c + _mm(dneg, neg)
        g_re, g_im = gq[:, :half], gq[:, half:]
        if g < own_groups:
            rterm = jnp.concatenate([g_re * w_re + g_im * w_im, g_im * w_re - g_re * w_im], axis=1)
            slot_sum = slot_sum + _spread(_select_t(srow[:, t0:t0 + block], slots), rterm)
        wterm = jnp.concatenate([g_re * r_re + g_im * r_im, g_im * r_re - g_re * r_im], axis=1)
        word_out[...] += _spread(word_t, wterm)
        neg_weight = lax.dot_general(neg_t, dneg, (((1,), (1,)), ((), ())),
                                     preferred_element_type=jnp.float32)
        ctx_out[...] += _spread(ctx_t, dpos * qf) + _spread(neg_weight, q)
    if own_groups:
        hit = orow[...] == lax.broadcasted_iota(jnp.int32, (rows, orow.shape[1]), 0)
        live_t = jnp.where(hit, live[...], 0.0).astype(jnp.bfloat16)
        slot_sum = slot_sum + 0.02 * _pick(live_t, table[...])
    kept = slot_out.shape[1] // 2
    slot_out[:, :kept] = slot_sum[:, :kept].astype(slot_out.dtype)
    slot_out[:, kept:] = slot_sum[:, half:half + kept].astype(slot_out.dtype)


def block_chains(word_ids, ctx_ids, slot_ids, own_ids, neg_ids, own_groups, scale, words, held,
                 table, own_rows, live_mask, row_width):
    trips = word_ids.shape[0]
    groups, neg_count = neg_ids.shape
    block = trips // groups
    parts, width = words.shape
    body = functools.partial(_chain_body, groups, own_groups, block, neg_count, scale)
    return pl.pallas_call(
        body,
        out_shape=(
            jax.ShapeDtypeStruct((parts, width), jnp.float32),
            jax.ShapeDtypeStruct((parts, width), jnp.float32),
            jax.ShapeDtypeStruct((own_rows.shape[0], row_width), jnp.float32),
        ),
        compiler_params=pltpu.CompilerParams(vmem_limit_bytes=48 * 1024 * 1024),
    )(
        word_ids.reshape(1, -1),
        ctx_ids.reshape(1, -1),
        slot_ids.reshape(1, -1),
        own_ids.reshape(1, -1),
        neg_ids,
        own_rows.reshape(1, -1),
        live_mask.reshape(1, -1),
        words,
        held,
        table,
    )


def lanes_of(half_width):
    return -(-half_width // 128) * 128


def padded_halves(rows, half_width):
    count = rows.shape[0]
    lanes = lanes_of(half_width)
    return jnp.pad(
        rows.reshape(count, 2, half_width), ((0, 0), (0, 0), (0, lanes - half_width))
    ).reshape(count, 2 * lanes)


def unpadded_halves(rows, half_width):
    count = rows.shape[0]
    return rows.reshape(count, 2, lanes_of(half_width))[:, :, :half_width].reshape(
        count, 2 * half_width
    )


def shards(
    words, contexts, relations, word_index, context_index, rel_slot, neg_index, requests, counts
):
    row_width = words.shape[1]
    half_width = row_width // 2
    part_count = lax.axis_size("blk")
    split_count = lax.axis_size("rel")
    owner_count = part_count * split_count
    slot_count = requests.shape[-1]
    slot_total = owner_count * slot_count
    owned_rows = relations.shape[0]
    part_rows = contexts.shape[0]
    trips = word_index.shape[0]
    block_count = neg_index.shape[0]
    neg_count = neg_index.shape[1]
    block_size = trips // block_count
    neg_scale = float(neg_count) ** (-0.5)
    both = ("blk", "rel")

    held_rows = passed_along(contexts, "blk", 1)

    own_ints = jnp.concatenate([word_index, context_index, rel_slot, neg_index.reshape(-1)])
    bucket_ints = jnp.stack(
        [own_ints] + [passed_along(own_ints, "rel", -j) for j in range(1, split_count)]
    )
    word_ids = bucket_ints[:, :trips].reshape(-1)
    ctx_ids = bucket_ints[:, trips : 2 * trips].reshape(-1)
    slot_ids = bucket_ints[:, 2 * trips : 3 * trips]
    slot_ids = (
        (slot_ids // slot_count) * (split_count * slot_count)
        + (jnp.arange(split_count) * slot_count)[:, None]
        + slot_ids % slot_count
    ).reshape(-1)
    own_slots = jnp.arange(slot_total)
    own_rows = (own_slots // slot_count) * (split_count * slot_count) + own_slots % slot_count
    neg_ids = bucket_ints[:, 3 * trips :].reshape(split_count * block_count, neg_count)

    wanted = requests[0, 0].reshape(owner_count, slot_count)
    incoming = lax.all_to_all(wanted, both, split_axis=0, concat_axis=0, tiled=True)
    lists = incoming.reshape(part_count, split_count, slot_count)
    served = jnp.stack([jnp.roll(lists, -j, axis=1) for j in range(split_count)], axis=2)
    padded_width = 2 * lanes_of(half_width)
    picked = jnp.einsum(
        "dkr,rf->dkf",
        one_hot(served.reshape(owner_count, split_count * slot_count), owned_rows),
        relations,
        preferred_element_type=jnp.float32,
    ).astype(jnp.bfloat16)
    fetched = lax.all_to_all(picked, both, split_axis=0, concat_axis=0, tiled=True)
    live_mask = (
        (jnp.arange(slot_count)[None, :] < counts[0, 0].reshape(owner_count)[:, None])
        .reshape(-1)
        .astype(jnp.float32)
    )

    group_count = split_count * block_count
    word_table = padded_halves(words, half_width)
    held_table = padded_halves(held_rows, half_width)
    fetched, word_table, held_table = lax.optimization_barrier((fetched, word_table, held_table))
    rel_table = padded_halves(fetched.reshape(split_count * slot_total, row_width), half_width)
    own_word, own_ctx, own_slot = block_chains(
        word_ids[:trips], ctx_ids[:trips], slot_ids[:trips], rel_slot, neg_ids[:block_count],
        block_count, neg_scale, word_table, held_table, rel_table, own_rows, live_mask,
        row_width,
    )
    rest_word, rest_ctx, _ = block_chains(
        word_ids[trips:], ctx_ids[trips:], slot_ids[trips:], rel_slot, neg_ids[block_count:],
        0, neg_scale, word_table, held_table, rel_table, own_rows[:8], live_mask[:8],
        row_width,
    )
    word_sum = unpadded_halves(own_word + rest_word, half_width)
    ctx_sum = unpadded_halves(own_ctx + rest_ctx, half_width)
    returned = lax.all_to_all(
        own_slot.astype(jnp.bfloat16).reshape(owner_count, slot_count, row_width),
        both,
        split_axis=0,
        concat_axis=0,
        tiled=True,
    ).astype(jnp.float32)
    incoming, returned = lax.optimization_barrier((incoming, returned))
    owner_map = (incoming.reshape(-1)[None, :] == jnp.arange(owned_rows)[:, None]).astype(
        jnp.float32
    )
    relation_grad = jnp.dot(
        owner_map,
        returned.reshape(-1, row_width),
        precision=lax.Precision.HIGHEST,
        preferred_element_type=jnp.float32,
    )
    return (word_sum.astype(jnp.bfloat16), ctx_sum.astype(jnp.bfloat16), relation_grad)


def solution(mesh):
    return jax.shard_map(
        shards,
        mesh=mesh,
        in_specs=(
            P("blk", None),
            P("blk", None),
            P(("blk", "rel"), None),
            P(("blk", "rel")),
            P(("blk", "rel")),
            P(("blk", "rel")),
            P(("blk", "rel"), None),
            P("blk", "rel", None, None, None),
            P("blk", "rel", None, None),
        ),
        out_specs=(P("blk", None), P("blk", None), P(("blk", "rel"), None)),
        check_vma=False,
    )
```

```python
import jax
import jax.numpy as jnp
from jax import lax
from jax.sharding import PartitionSpec as P
import functools
from jax.experimental import pallas as pl
from jax.experimental.pallas import tpu as pltpu


def passed_along(shard, axis, by):
    length = lax.axis_size(axis)
    return lax.ppermute(shard, axis, [(i, (i + by) % length) for i in range(length)])


def complex_product(left_vec, right_vec, half_width):
    left_re, left_im = (left_vec[..., :half_width], left_vec[..., half_width:])
    right_re, right_im = (right_vec[..., :half_width], right_vec[..., half_width:])
    return jnp.concatenate(
        [left_re * right_re - left_im * right_im, left_re * right_im + left_im * right_re], axis=-1
    )


def conj_product(grad_vec, other_vec, half_width):
    grad_re, grad_im = (grad_vec[..., :half_width], grad_vec[..., half_width:])
    other_re, other_im = (other_vec[..., :half_width], other_vec[..., half_width:])
    return jnp.concatenate(
        [grad_re * other_re + grad_im * other_im, grad_im * other_re - grad_re * other_im], axis=-1
    )


def one_hot(index_ids, row_total):
    return (index_ids[..., None] == jnp.arange(row_total)).astype(jnp.bfloat16)


def pick_rows(selector, rows):
    return jnp.dot(selector, rows, preferred_element_type=jnp.float32)


def split_bf16(values):
    upper = values.astype(jnp.bfloat16)
    lower = (values - upper.astype(jnp.float32)).astype(jnp.bfloat16)
    return upper, lower


def spread_rows(selector, terms):
    upper, lower = split_bf16(terms)
    dims = (((0,), (0,)), ((), ()))
    return lax.dot_general(
        selector, upper, dims, preferred_element_type=jnp.float32
    ) + lax.dot_general(selector, lower, dims, preferred_element_type=jnp.float32)


def _sigmoid(x):
    return 1.0 / (1.0 + jnp.exp(-x))


def _select_t(ids_row, total):
    hit = ids_row == lax.broadcasted_iota(jnp.int32, (total, ids_row.shape[1]), 0)
    return jnp.where(hit, 1.0, 0.0).astype(jnp.bfloat16)


def _mm(a, b):
    return jnp.dot(a, b, preferred_element_type=jnp.float32)


def _pick(sel_t, rows):
    return lax.dot_general(sel_t, rows, (((0,), (0,)), ((), ())),
                           preferred_element_type=jnp.float32)


def _spread(sel_t, terms):
    upper = terms.astype(jnp.bfloat16)
    lower = (terms - upper.astype(jnp.float32)).astype(jnp.bfloat16)
    return _mm(sel_t, upper) + _mm(sel_t, lower)


def _chain_body(groups, own_groups, block, neg_count, scale,
                wrow, crow, scomb, srow, nrow, orow, live,
                words, held, table, word_out, ctx_out, slot_out):
    parts = words.shape[0]
    rows = table.shape[0]
    slots = slot_out.shape[0]
    half = words.shape[1] // 2
    word_out[...] = jnp.zeros(word_out.shape, jnp.float32)
    ctx_out[...] = jnp.zeros(ctx_out.shape, jnp.float32)
    slot_sum = jnp.zeros((slot_out.shape[0], words.shape[1]), jnp.float32)
    for g in range(groups):
        t0 = g * block
        word_t = _select_t(wrow[:, t0:t0 + block], parts)
        ctx_t = _select_t(crow[:, t0:t0 + block], parts)
        w = _pick(word_t, words[...])
        c = _pick(ctx_t, held[...])
        rv = _pick(_select_t(scomb[:, t0:t0 + block], rows), table[...])
        w_re, w_im = w[:, :half], w[:, half:]
        r_re, r_im = rv[:, :half], rv[:, half:]
        q = jnp.concatenate([w_re * r_re - w_im * r_im, w_re * r_im + w_im * r_re], axis=1)
        q = q.astype(jnp.bfloat16)
        qf = q.astype(jnp.float32)
        pos = jnp.sum(qf * c, axis=1, keepdims=True)
        dpos = -1.0 / (1.0 + jnp.exp(pos))
        neg_t = _select_t(nrow[g:g + 1, :], parts)
        neg = _pick(neg_t, held[...]).astype(jnp.bfloat16)
        scores = lax.dot_general(q, neg, (((1,), (1,)), ((), ())),
                                 preferred_element_type=jnp.float32)
        dneg = (_sigmoid(scores) * scale).astype(jnp.bfloat16)
        gq = dpos * c + _mm(dneg, neg)
        g_re, g_im = gq[:, :half], gq[:, half:]
        if g < own_groups:
            rterm = jnp.concatenate([g_re * w_re + g_im * w_im, g_im * w_re - g_re * w_im], axis=1)
            slot_sum = slot_sum + _spread(_select_t(srow[:, t0:t0 + block], slots), rterm)
        wterm = jnp.concatenate([g_re * r_re + g_im * r_im, g_im * r_re - g_re * r_im], axis=1)
        word_out[...] += _spread(word_t, wterm)
        neg_weight = lax.dot_general(neg_t, dneg, (((1,), (1,)), ((), ())),
                                     preferred_element_type=jnp.float32)
        ctx_out[...] += _spread(ctx_t, dpos * qf) + _spread(neg_weight, q)
    if own_groups:
        hit = orow[...] == lax.broadcasted_iota(jnp.int32, (rows, orow.shape[1]), 0)
        live_t = jnp.where(hit, live[...], 0.0).astype(jnp.bfloat16)
        slot_sum = slot_sum + 0.02 * _pick(live_t, table[...])
    kept = slot_out.shape[1] // 2
    slot_out[:, :kept] = slot_sum[:, :kept].astype(slot_out.dtype)
    slot_out[:, kept:] = slot_sum[:, half:half + kept].astype(slot_out.dtype)


def block_chains(word_ids, ctx_ids, slot_ids, own_ids, neg_ids, own_groups, scale, words, held,
                 table, own_rows, live_mask, row_width):
    trips = word_ids.shape[0]
    groups, neg_count = neg_ids.shape
    block = trips // groups
    parts, width = words.shape
    body = functools.partial(_chain_body, groups, own_groups, block, neg_count, scale)
    return pl.pallas_call(
        body,
        out_shape=(
            jax.ShapeDtypeStruct((parts, width), jnp.float32),
            jax.ShapeDtypeStruct((parts, width), jnp.float32),
            jax.ShapeDtypeStruct((own_rows.shape[0], row_width), jnp.float32),
        ),
        compiler_params=pltpu.CompilerParams(vmem_limit_bytes=48 * 1024 * 1024),
    )(
        word_ids.reshape(1, -1),
        ctx_ids.reshape(1, -1),
        slot_ids.reshape(1, -1),
        own_ids.reshape(1, -1),
        neg_ids,
        own_rows.reshape(1, -1),
        live_mask.reshape(1, -1),
        words,
        held,
        table,
    )


def lanes_of(half_width):
    return -(-half_width // 128) * 128


def padded_halves(rows, half_width):
    count = rows.shape[0]
    lanes = lanes_of(half_width)
    return jnp.pad(
        rows.reshape(count, 2, half_width), ((0, 0), (0, 0), (0, lanes - half_width))
    ).reshape(count, 2 * lanes)


def unpadded_halves(rows, half_width):
    count = rows.shape[0]
    return rows.reshape(count, 2, lanes_of(half_width))[:, :, :half_width].reshape(
        count, 2 * half_width
    )


def shards(
    words, contexts, relations, word_index, context_index, rel_slot, neg_index, requests, counts
):
    row_width = words.shape[1]
    half_width = row_width // 2
    part_count = lax.axis_size("blk")
    split_count = lax.axis_size("rel")
    owner_count = part_count * split_count
    slot_count = requests.shape[-1]
    slot_total = owner_count * slot_count
    owned_rows = relations.shape[0]
    part_rows = contexts.shape[0]
    trips = word_index.shape[0]
    block_count = neg_index.shape[0]
    neg_count = neg_index.shape[1]
    block_size = trips // block_count
    neg_scale = float(neg_count) ** (-0.5)
    both = ("blk", "rel")

    held_rows = passed_along(contexts, "blk", 1)

    own_ints = jnp.concatenate([word_index, context_index, rel_slot, neg_index.reshape(-1)])
    bucket_ints = jnp.stack(
        [own_ints] + [passed_along(own_ints, "rel", -j) for j in range(1, split_count)]
    )
    word_ids = bucket_ints[:, :trips].reshape(-1)
    ctx_ids = bucket_ints[:, trips : 2 * trips].reshape(-1)
    slot_ids = bucket_ints[:, 2 * trips : 3 * trips]
    slot_ids = (
        (slot_ids // slot_count) * (split_count * slot_count)
        + (jnp.arange(split_count) * slot_count)[:, None]
        + slot_ids % slot_count
    ).reshape(-1)
    own_slots = jnp.arange(slot_total)
    own_rows = (own_slots // slot_count) * (split_count * slot_count) + own_slots % slot_count
    neg_ids = bucket_ints[:, 3 * trips :].reshape(split_count * block_count, neg_count)

    wanted = requests[0, 0].reshape(owner_count, slot_count)
    incoming = lax.all_to_all(wanted, both, split_axis=0, concat_axis=0, tiled=True)
    lists = incoming.reshape(part_count, split_count, slot_count)
    served = jnp.stack([jnp.roll(lists, -j, axis=1) for j in range(split_count)], axis=2)
    padded_width = 2 * lanes_of(half_width)
    picked = jnp.einsum(
        "dkr,rf->dkf",
        one_hot(served.reshape(owner_count, split_count * slot_count), owned_rows),
        relations,
        preferred_element_type=jnp.float32,
    ).astype(jnp.bfloat16)
    fetched = lax.all_to_all(picked, both, split_axis=0, concat_axis=0, tiled=True)
    live_mask = (
        (jnp.arange(slot_count)[None, :] < counts[0, 0].reshape(owner_count)[:, None])
        .reshape(-1)
        .astype(jnp.float32)
    )

    group_count = split_count * block_count
    word_table = padded_halves(words, half_width)
    held_table = padded_halves(held_rows, half_width)
    fetched, word_table, held_table = lax.optimization_barrier((fetched, word_table, held_table))
    rel_table = padded_halves(fetched.reshape(split_count * slot_total, row_width), half_width)
    own_word, own_ctx, own_slot = block_chains(
        word_ids[:trips], ctx_ids[:trips], slot_ids[:trips], rel_slot, neg_ids[:block_count],
        block_count, neg_scale, word_table, held_table, rel_table, own_rows, live_mask,
        row_width,
    )
    rest_word, rest_ctx, _ = block_chains(
        word_ids[trips:], ctx_ids[trips:], slot_ids[trips:], rel_slot, neg_ids[block_count:],
        0, neg_scale, word_table, held_table, rel_table, own_rows[:8], live_mask[:8],
        row_width,
    )
    word_sum = unpadded_halves(own_word + rest_word, half_width)
    ctx_sum = unpadded_halves(own_ctx + rest_ctx, half_width)
    returned = lax.all_to_all(
        own_slot.astype(jnp.bfloat16).reshape(owner_count, slot_count, row_width),
        both,
        split_axis=0,
        concat_axis=0,
        tiled=True,
    )
    incoming, returned = lax.optimization_barrier((incoming, returned))
    owner_map = one_hot(incoming.reshape(owner_count, slot_count), owned_rows)
    relation_grad = jnp.einsum(
        "dkr,dkf->rf", owner_map, returned, preferred_element_type=jnp.float32
    )
    return (word_sum.astype(jnp.bfloat16), ctx_sum.astype(jnp.bfloat16), relation_grad)


def solution(mesh):
    return jax.shard_map(
        shards,
        mesh=mesh,
        in_specs=(
            P("blk", None),
            P("blk", None),
            P(("blk", "rel"), None),
            P(("blk", "rel")),
            P(("blk", "rel")),
            P(("blk", "rel")),
            P(("blk", "rel"), None),
            P("blk", "rel", None, None, None),
            P("blk", "rel", None, None),
        ),
        out_specs=(P("blk", None), P("blk", None), P(("blk", "rel"), None)),
        check_vma=False,
    )
```

```python
import jax
import jax.numpy as jnp
from jax import lax
from jax.sharding import PartitionSpec as P
import functools
from jax.experimental import pallas as pl
from jax.experimental.pallas import tpu as pltpu


def passed_along(shard, axis, by):
    length = lax.axis_size(axis)
    return lax.ppermute(shard, axis, [(i, (i + by) % length) for i in range(length)])


def complex_product(left_vec, right_vec, half_width):
    left_re, left_im = (left_vec[..., :half_width], left_vec[..., half_width:])
    right_re, right_im = (right_vec[..., :half_width], right_vec[..., half_width:])
    return jnp.concatenate(
        [left_re * right_re - left_im * right_im, left_re * right_im + left_im * right_re], axis=-1
    )


def conj_product(grad_vec, other_vec, half_width):
    grad_re, grad_im = (grad_vec[..., :half_width], grad_vec[..., half_width:])
    other_re, other_im = (other_vec[..., :half_width], other_vec[..., half_width:])
    return jnp.concatenate(
        [grad_re * other_re + grad_im * other_im, grad_im * other_re - grad_re * other_im], axis=-1
    )


def one_hot(index_ids, row_total):
    return (index_ids[..., None] == jnp.arange(row_total)).astype(jnp.bfloat16)


def pick_rows(selector, rows):
    return jnp.dot(selector, rows, preferred_element_type=jnp.float32)


def split_bf16(values):
    upper = values.astype(jnp.bfloat16)
    lower = (values - upper.astype(jnp.float32)).astype(jnp.bfloat16)
    return upper, lower


def spread_rows(selector, terms):
    upper, lower = split_bf16(terms)
    dims = (((0,), (0,)), ((), ()))
    return lax.dot_general(
        selector, upper, dims, preferred_element_type=jnp.float32
    ) + lax.dot_general(selector, lower, dims, preferred_element_type=jnp.float32)


def _sigmoid(x):
    return 1.0 / (1.0 + jnp.exp(-x))


def _select_t(ids_row, total):
    hit = ids_row == lax.broadcasted_iota(jnp.int32, (total, ids_row.shape[1]), 0)
    return jnp.where(hit, 1.0, 0.0).astype(jnp.bfloat16)


def _mm(a, b):
    return jnp.dot(a, b, preferred_element_type=jnp.float32)


def _pick(sel_t, rows):
    return lax.dot_general(sel_t, rows, (((0,), (0,)), ((), ())),
                           preferred_element_type=jnp.float32)


def _spread(sel_t, terms):
    upper = terms.astype(jnp.bfloat16)
    lower = (terms - upper.astype(jnp.float32)).astype(jnp.bfloat16)
    return _mm(sel_t, upper) + _mm(sel_t, lower)


def _chain_body(groups, own_groups, block, neg_count, scale,
                wrow, crow, scomb, srow, nrow, orow, live,
                words, held, table, word_out, ctx_out, slot_out):
    parts = words.shape[0]
    rows = table.shape[0]
    slots = slot_out.shape[0]
    half = words.shape[1] // 2
    word_out[...] = jnp.zeros(word_out.shape, jnp.float32)
    ctx_out[...] = jnp.zeros(ctx_out.shape, jnp.float32)
    slot_sum = jnp.zeros((slot_out.shape[0], words.shape[1]), jnp.float32)
    for g in range(groups):
        t0 = g * block
        word_t = _select_t(wrow[:, t0:t0 + block], parts)
        ctx_t = _select_t(crow[:, t0:t0 + block], parts)
        w = _pick(word_t, words[...])
        c = _pick(ctx_t, held[...])
        rv = _pick(_select_t(scomb[:, t0:t0 + block], rows), table[...])
        w_re, w_im = w[:, :half], w[:, half:]
        r_re, r_im = rv[:, :half], rv[:, half:]
        q = jnp.concatenate([w_re * r_re - w_im * r_im, w_re * r_im + w_im * r_re], axis=1)
        q = q.astype(jnp.bfloat16)
        qf = q.astype(jnp.float32)
        pos = jnp.sum(qf * c, axis=1, keepdims=True)
        dpos = -1.0 / (1.0 + jnp.exp(pos))
        neg_t = _select_t(nrow[g:g + 1, :], parts)
        neg = _pick(neg_t, held[...]).astype(jnp.bfloat16)
        scores = lax.dot_general(q, neg, (((1,), (1,)), ((), ())),
                                 preferred_element_type=jnp.float32)
        dneg = (_sigmoid(scores) * scale).astype(jnp.bfloat16)
        gq = dpos * c + _mm(dneg, neg)
        g_re, g_im = gq[:, :half], gq[:, half:]
        if g < own_groups:
            rterm = jnp.concatenate([g_re * w_re + g_im * w_im, g_im * w_re - g_re * w_im], axis=1)
            slot_sum = slot_sum + _spread(_select_t(srow[:, t0:t0 + block], slots), rterm)
        wterm = jnp.concatenate([g_re * r_re + g_im * r_im, g_im * r_re - g_re * r_im], axis=1)
        word_out[...] += _spread(word_t, wterm)
        neg_weight = lax.dot_general(neg_t, dneg, (((1,), (1,)), ((), ())),
                                     preferred_element_type=jnp.float32)
        ctx_out[...] += _spread(ctx_t, dpos * qf) + _spread(neg_weight, q)
    if own_groups:
        hit = orow[...] == lax.broadcasted_iota(jnp.int32, (rows, orow.shape[1]), 0)
        live_t = jnp.where(hit, live[...], 0.0).astype(jnp.bfloat16)
        slot_sum = slot_sum + 0.02 * _pick(live_t, table[...])
    kept = slot_out.shape[1] // 2
    slot_out[:, :kept] = slot_sum[:, :kept].astype(slot_out.dtype)
    slot_out[:, kept:] = slot_sum[:, half:half + kept].astype(slot_out.dtype)


def block_chains(word_ids, ctx_ids, slot_ids, own_ids, neg_ids, own_groups, scale, words, held,
                 table, own_rows, live_mask, row_width):
    trips = word_ids.shape[0]
    groups, neg_count = neg_ids.shape
    block = trips // groups
    parts, width = words.shape
    body = functools.partial(_chain_body, groups, own_groups, block, neg_count, scale)
    return pl.pallas_call(
        body,
        out_shape=(
            jax.ShapeDtypeStruct((parts, width), jnp.float32),
            jax.ShapeDtypeStruct((parts, width), jnp.float32),
            jax.ShapeDtypeStruct((own_rows.shape[0], row_width), jnp.float32),
        ),
        compiler_params=pltpu.CompilerParams(vmem_limit_bytes=48 * 1024 * 1024),
    )(
        word_ids.reshape(1, -1),
        ctx_ids.reshape(1, -1),
        slot_ids.reshape(1, -1),
        own_ids.reshape(1, -1),
        neg_ids,
        own_rows.reshape(1, -1),
        live_mask.reshape(1, -1),
        words,
        held,
        table,
    )


def lanes_of(half_width):
    return -(-half_width // 128) * 128


def padded_halves(rows, half_width):
    count = rows.shape[0]
    lanes = lanes_of(half_width)
    return jnp.pad(
        rows.reshape(count, 2, half_width), ((0, 0), (0, 0), (0, lanes - half_width))
    ).reshape(count, 2 * lanes)


def unpadded_halves(rows, half_width):
    count = rows.shape[0]
    return rows.reshape(count, 2, lanes_of(half_width))[:, :, :half_width].reshape(
        count, 2 * half_width
    )


def shards(
    words, contexts, relations, word_index, context_index, rel_slot, neg_index, requests, counts
):
    row_width = words.shape[1]
    half_width = row_width // 2
    part_count = lax.axis_size("blk")
    split_count = lax.axis_size("rel")
    owner_count = part_count * split_count
    slot_count = requests.shape[-1]
    slot_total = owner_count * slot_count
    owned_rows = relations.shape[0]
    part_rows = contexts.shape[0]
    trips = word_index.shape[0]
    block_count = neg_index.shape[0]
    neg_count = neg_index.shape[1]
    block_size = trips // block_count
    neg_scale = float(neg_count) ** (-0.5)
    both = ("blk", "rel")

    held_rows = passed_along(contexts, "blk", 1)

    own_ints = jnp.concatenate([word_index, context_index, rel_slot, neg_index.reshape(-1)])
    bucket_ints = jnp.stack(
        [own_ints] + [passed_along(own_ints, "rel", -j) for j in range(1, split_count)]
    )
    word_ids = bucket_ints[:, :trips].reshape(-1)
    ctx_ids = bucket_ints[:, trips : 2 * trips].reshape(-1)
    slot_ids = bucket_ints[:, 2 * trips : 3 * trips]
    list_of = (lax.axis_index("rel") + jnp.arange(split_count)) % split_count
    slot_ids = (
        (slot_ids // slot_count) * (split_count * slot_count)
        + (list_of * slot_count)[:, None]
        + slot_ids % slot_count
    ).reshape(-1)
    own_slots = jnp.arange(slot_total)
    own_rows = (
        (own_slots // slot_count) * (split_count * slot_count)
        + list_of[0] * slot_count
        + own_slots % slot_count
    )
    neg_ids = bucket_ints[:, 3 * trips :].reshape(split_count * block_count, neg_count)

    wanted = requests[0, 0].reshape(owner_count, slot_count)
    incoming = lax.all_to_all(wanted, both, split_axis=0, concat_axis=0, tiled=True)
    lists = incoming.reshape(part_count, split_count, slot_count)
    served = jnp.broadcast_to(
        lists[:, None], (part_count, split_count, split_count, slot_count)
    )
    padded_width = 2 * lanes_of(half_width)
    picked = jnp.einsum(
        "dkr,rf->dkf",
        one_hot(served.reshape(owner_count, split_count * slot_count), owned_rows),
        relations,
        preferred_element_type=jnp.float32,
    ).astype(jnp.bfloat16)
    fetched = lax.all_to_all(picked, both, split_axis=0, concat_axis=0, tiled=True)
    live_mask = (
        (jnp.arange(slot_count)[None, :] < counts[0, 0].reshape(owner_count)[:, None])
        .reshape(-1)
        .astype(jnp.float32)
    )

    group_count = split_count * block_count
    word_table = padded_halves(words, half_width)
    held_table = padded_halves(held_rows, half_width)
    fetched, word_table, held_table = lax.optimization_barrier((fetched, word_table, held_table))
    rel_table = padded_halves(fetched.reshape(split_count * slot_total, row_width), half_width)
    own_word, own_ctx, own_slot = block_chains(
        word_ids[:trips], ctx_ids[:trips], slot_ids[:trips], rel_slot, neg_ids[:block_count],
        block_count, neg_scale, word_table, held_table, rel_table, own_rows, live_mask,
        row_width,
    )
    rest_word, rest_ctx, _ = block_chains(
        word_ids[trips:], ctx_ids[trips:], slot_ids[trips:], rel_slot, neg_ids[block_count:],
        0, neg_scale, word_table, held_table, rel_table, own_rows[:8], live_mask[:8],
        row_width,
    )
    word_sum = unpadded_halves(own_word + rest_word, half_width)
    ctx_sum = unpadded_halves(own_ctx + rest_ctx, half_width)
    returned = lax.all_to_all(
        own_slot.astype(jnp.bfloat16).reshape(owner_count, slot_count, row_width),
        both,
        split_axis=0,
        concat_axis=0,
        tiled=True,
    )
    incoming, returned = lax.optimization_barrier((incoming, returned))
    owner_map = one_hot(incoming.reshape(owner_count, slot_count), owned_rows)
    relation_grad = jnp.einsum(
        "dkr,dkf->rf", owner_map, returned, preferred_element_type=jnp.float32
    )
    return (word_sum.astype(jnp.bfloat16), ctx_sum.astype(jnp.bfloat16), relation_grad)


def solution(mesh):
    return jax.shard_map(
        shards,
        mesh=mesh,
        in_specs=(
            P("blk", None),
            P("blk", None),
            P(("blk", "rel"), None),
            P(("blk", "rel")),
            P(("blk", "rel")),
            P(("blk", "rel")),
            P(("blk", "rel"), None),
            P("blk", "rel", None, None, None),
            P("blk", "rel", None, None),
        ),
        out_specs=(P("blk", None), P("blk", None), P(("blk", "rel"), None)),
        check_vma=False,
    )
```

```python
import jax
import jax.numpy as jnp
from jax import lax
from jax.sharding import PartitionSpec as P
import functools
from jax.experimental import pallas as pl
from jax.experimental.pallas import tpu as pltpu


def passed_along(shard, axis, by):
    length = lax.axis_size(axis)
    return lax.ppermute(shard, axis, [(i, (i + by) % length) for i in range(length)])


def complex_product(left_vec, right_vec, half_width):
    left_re, left_im = (left_vec[..., :half_width], left_vec[..., half_width:])
    right_re, right_im = (right_vec[..., :half_width], right_vec[..., half_width:])
    return jnp.concatenate(
        [left_re * right_re - left_im * right_im, left_re * right_im + left_im * right_re], axis=-1
    )


def conj_product(grad_vec, other_vec, half_width):
    grad_re, grad_im = (grad_vec[..., :half_width], grad_vec[..., half_width:])
    other_re, other_im = (other_vec[..., :half_width], other_vec[..., half_width:])
    return jnp.concatenate(
        [grad_re * other_re + grad_im * other_im, grad_im * other_re - grad_re * other_im], axis=-1
    )


def one_hot(index_ids, row_total):
    return (index_ids[..., None] == jnp.arange(row_total)).astype(jnp.bfloat16)


def pick_rows(selector, rows):
    return jnp.dot(selector, rows, preferred_element_type=jnp.float32)


def split_bf16(values):
    upper = values.astype(jnp.bfloat16)
    lower = (values - upper.astype(jnp.float32)).astype(jnp.bfloat16)
    return upper, lower


def spread_rows(selector, terms):
    upper, lower = split_bf16(terms)
    dims = (((0,), (0,)), ((), ()))
    return lax.dot_general(
        selector, upper, dims, preferred_element_type=jnp.float32
    ) + lax.dot_general(selector, lower, dims, preferred_element_type=jnp.float32)


def _sigmoid(x):
    return 1.0 / (1.0 + jnp.exp(-x))


def _select_t(ids_row, total):
    hit = ids_row == lax.broadcasted_iota(jnp.int32, (total, ids_row.shape[1]), 0)
    return jnp.where(hit, 1.0, 0.0).astype(jnp.bfloat16)


def _mm(a, b):
    return jnp.dot(a, b, preferred_element_type=jnp.float32)


def _pick(sel_t, rows):
    return lax.dot_general(sel_t, rows, (((0,), (0,)), ((), ())),
                           preferred_element_type=jnp.float32)


def _spread(sel_t, terms):
    upper = terms.astype(jnp.bfloat16)
    lower = (terms - upper.astype(jnp.float32)).astype(jnp.bfloat16)
    return _mm(sel_t, upper) + _mm(sel_t, lower)


def _chain_body(groups, own_groups, block, neg_count, scale, accumulate, *refs):
    wrow, crow, scomb, srow, nrow, orow, live, words, held, table = refs[:10]
    word_out, ctx_out, slot_out = refs[-3:]
    parts = words.shape[0]
    rows = table.shape[0]
    slots = slot_out.shape[0]
    half = words.shape[1] // 2
    if not accumulate:
        word_out[...] = jnp.zeros(word_out.shape, jnp.float32)
        ctx_out[...] = jnp.zeros(ctx_out.shape, jnp.float32)
    slot_sum = jnp.zeros((slot_out.shape[0], words.shape[1]), jnp.float32)
    for g in range(groups):
        t0 = g * block
        word_t = _select_t(wrow[:, t0:t0 + block], parts)
        ctx_t = _select_t(crow[:, t0:t0 + block], parts)
        w = _pick(word_t, words[...])
        c = _pick(ctx_t, held[...])
        rv = _pick(_select_t(scomb[:, t0:t0 + block], rows), table[...])
        w_re, w_im = w[:, :half], w[:, half:]
        r_re, r_im = rv[:, :half], rv[:, half:]
        q = jnp.concatenate([w_re * r_re - w_im * r_im, w_re * r_im + w_im * r_re], axis=1)
        q = q.astype(jnp.bfloat16)
        qf = q.astype(jnp.float32)
        pos = jnp.sum(qf * c, axis=1, keepdims=True)
        dpos = -1.0 / (1.0 + jnp.exp(pos))
        neg_t = _select_t(nrow[g:g + 1, :], parts)
        neg = _pick(neg_t, held[...]).astype(jnp.bfloat16)
        scores = lax.dot_general(q, neg, (((1,), (1,)), ((), ())),
                                 preferred_element_type=jnp.float32)
        dneg = (_sigmoid(scores) * scale).astype(jnp.bfloat16)
        gq = dpos * c + _mm(dneg, neg)
        g_re, g_im = gq[:, :half], gq[:, half:]
        if g < own_groups:
            rterm = jnp.concatenate([g_re * w_re + g_im * w_im, g_im * w_re - g_re * w_im], axis=1)
            slot_sum = slot_sum + _spread(_select_t(srow[:, t0:t0 + block], slots), rterm)
        wterm = jnp.concatenate([g_re * r_re + g_im * r_im, g_im * r_re - g_re * r_im], axis=1)
        word_out[...] += _spread(word_t, wterm)
        neg_weight = lax.dot_general(neg_t, dneg, (((1,), (1,)), ((), ())),
                                     preferred_element_type=jnp.float32)
        ctx_out[...] += _spread(ctx_t, dpos * qf) + _spread(neg_weight, q)
    if own_groups:
        hit = orow[...] == lax.broadcasted_iota(jnp.int32, (rows, orow.shape[1]), 0)
        live_t = jnp.where(hit, live[...], 0.0).astype(jnp.bfloat16)
        slot_sum = slot_sum + 0.02 * _pick(live_t, table[...])
    kept = slot_out.shape[1] // 2
    slot_out[:, :kept] = slot_sum[:, :kept].astype(slot_out.dtype)
    slot_out[:, kept:] = slot_sum[:, half:half + kept].astype(slot_out.dtype)


def block_chains(word_ids, ctx_ids, slot_ids, own_ids, neg_ids, own_groups, scale, words, held,
                 table, own_rows, live_mask, row_width, totals=()):
    trips = word_ids.shape[0]
    groups, neg_count = neg_ids.shape
    block = trips // groups
    parts, width = words.shape
    body = functools.partial(
        _chain_body, groups, own_groups, block, neg_count, scale, bool(totals)
    )
    return pl.pallas_call(
        body,
        out_shape=(
            jax.ShapeDtypeStruct((parts, width), jnp.float32),
            jax.ShapeDtypeStruct((parts, width), jnp.float32),
            jax.ShapeDtypeStruct((own_rows.shape[0], row_width), jnp.float32),
        ),
        compiler_params=pltpu.CompilerParams(vmem_limit_bytes=48 * 1024 * 1024),
        input_output_aliases={10 + i: i for i in range(len(totals))},
    )(
        word_ids.reshape(1, -1),
        ctx_ids.reshape(1, -1),
        slot_ids.reshape(1, -1),
        own_ids.reshape(1, -1),
        neg_ids,
        own_rows.reshape(1, -1),
        live_mask.reshape(1, -1),
        words,
        held,
        table,
        *totals,
    )


def lanes_of(half_width):
    return -(-half_width // 128) * 128


def padded_halves(rows, half_width):
    count = rows.shape[0]
    lanes = lanes_of(half_width)
    return jnp.pad(
        rows.reshape(count, 2, half_width), ((0, 0), (0, 0), (0, lanes - half_width))
    ).reshape(count, 2 * lanes)


def unpadded_halves(rows, half_width):
    count = rows.shape[0]
    return rows.reshape(count, 2, lanes_of(half_width))[:, :, :half_width].reshape(
        count, 2 * half_width
    )


def shards(
    words, contexts, relations, word_index, context_index, rel_slot, neg_index, requests, counts
):
    row_width = words.shape[1]
    half_width = row_width // 2
    part_count = lax.axis_size("blk")
    split_count = lax.axis_size("rel")
    owner_count = part_count * split_count
    slot_count = requests.shape[-1]
    slot_total = owner_count * slot_count
    owned_rows = relations.shape[0]
    part_rows = contexts.shape[0]
    trips = word_index.shape[0]
    block_count = neg_index.shape[0]
    neg_count = neg_index.shape[1]
    block_size = trips // block_count
    neg_scale = float(neg_count) ** (-0.5)
    both = ("blk", "rel")

    held_rows = passed_along(contexts, "blk", 1)

    own_ints = jnp.concatenate([word_index, context_index, rel_slot, neg_index.reshape(-1)])
    bucket_ints = jnp.stack(
        [own_ints] + [passed_along(own_ints, "rel", -j) for j in range(1, split_count)]
    )
    word_ids = bucket_ints[:, :trips].reshape(-1)
    ctx_ids = bucket_ints[:, trips : 2 * trips].reshape(-1)
    slot_ids = bucket_ints[:, 2 * trips : 3 * trips]
    list_of = (lax.axis_index("rel") + jnp.arange(split_count)) % split_count
    slot_ids = (
        (slot_ids // slot_count) * (split_count * slot_count)
        + (list_of * slot_count)[:, None]
        + slot_ids % slot_count
    ).reshape(-1)
    own_slots = jnp.arange(slot_total)
    own_rows = (
        (own_slots // slot_count) * (split_count * slot_count)
        + list_of[0] * slot_count
        + own_slots % slot_count
    )
    neg_ids = bucket_ints[:, 3 * trips :].reshape(split_count * block_count, neg_count)

    wanted = requests[0, 0].reshape(owner_count, slot_count)
    incoming = lax.all_to_all(wanted, both, split_axis=0, concat_axis=0, tiled=True)
    lists = incoming.reshape(part_count, split_count, slot_count)
    served = jnp.broadcast_to(
        lists[:, None], (part_count, split_count, split_count, slot_count)
    )
    padded_width = 2 * lanes_of(half_width)
    picked = jnp.einsum(
        "dkr,rf->dkf",
        one_hot(served.reshape(owner_count, split_count * slot_count), owned_rows),
        relations,
        preferred_element_type=jnp.float32,
    ).astype(jnp.bfloat16)
    fetched = lax.all_to_all(picked, both, split_axis=0, concat_axis=0, tiled=True)
    live_mask = (
        (jnp.arange(slot_count)[None, :] < counts[0, 0].reshape(owner_count)[:, None])
        .reshape(-1)
        .astype(jnp.float32)
    )

    group_count = split_count * block_count
    word_table = padded_halves(words, half_width)
    held_table = padded_halves(held_rows, half_width)
    fetched, word_table, held_table = lax.optimization_barrier((fetched, word_table, held_table))
    rel_table = padded_halves(fetched.reshape(split_count * slot_total, row_width), half_width)
    own_word, own_ctx, own_slot = block_chains(
        word_ids[:trips], ctx_ids[:trips], slot_ids[:trips], rel_slot, neg_ids[:block_count],
        block_count, neg_scale, word_table, held_table, rel_table, own_rows, live_mask,
        row_width,
    )
    all_word, all_ctx, _ = block_chains(
        word_ids[trips:], ctx_ids[trips:], slot_ids[trips:], rel_slot, neg_ids[block_count:],
        0, neg_scale, word_table, held_table, rel_table, own_rows[:8], live_mask[:8],
        row_width, totals=(own_word, own_ctx),
    )
    word_sum = unpadded_halves(all_word, half_width)
    ctx_sum = unpadded_halves(all_ctx, half_width)
    returned = lax.all_to_all(
        own_slot.astype(jnp.bfloat16).reshape(owner_count, slot_count, row_width),
        both,
        split_axis=0,
        concat_axis=0,
        tiled=True,
    )
    incoming, returned = lax.optimization_barrier((incoming, returned))
    owner_map = one_hot(incoming.reshape(owner_count, slot_count), owned_rows)
    relation_grad = jnp.einsum(
        "dkr,dkf->rf", owner_map, returned, preferred_element_type=jnp.float32
    )
    return (word_sum.astype(jnp.bfloat16), ctx_sum.astype(jnp.bfloat16), relation_grad)


def solution(mesh):
    return jax.shard_map(
        shards,
        mesh=mesh,
        in_specs=(
            P("blk", None),
            P("blk", None),
            P(("blk", "rel"), None),
            P(("blk", "rel")),
            P(("blk", "rel")),
            P(("blk", "rel")),
            P(("blk", "rel"), None),
            P("blk", "rel", None, None, None),
            P("blk", "rel", None, None),
        ),
        out_specs=(P("blk", None), P("blk", None), P(("blk", "rel"), None)),
        check_vma=False,
    )
```

```python
import jax
import jax.numpy as jnp
from jax import lax
from jax.sharding import PartitionSpec as P
import functools
from jax.experimental import pallas as pl
from jax.experimental.pallas import tpu as pltpu


def passed_along(shard, axis, by):
    length = lax.axis_size(axis)
    return lax.ppermute(shard, axis, [(i, (i + by) % length) for i in range(length)])


def complex_product(left_vec, right_vec, half_width):
    left_re, left_im = (left_vec[..., :half_width], left_vec[..., half_width:])
    right_re, right_im = (right_vec[..., :half_width], right_vec[..., half_width:])
    return jnp.concatenate(
        [left_re * right_re - left_im * right_im, left_re * right_im + left_im * right_re], axis=-1
    )


def conj_product(grad_vec, other_vec, half_width):
    grad_re, grad_im = (grad_vec[..., :half_width], grad_vec[..., half_width:])
    other_re, other_im = (other_vec[..., :half_width], other_vec[..., half_width:])
    return jnp.concatenate(
        [grad_re * other_re + grad_im * other_im, grad_im * other_re - grad_re * other_im], axis=-1
    )


def one_hot(index_ids, row_total):
    return (index_ids[..., None] == jnp.arange(row_total)).astype(jnp.bfloat16)


def pick_rows(selector, rows):
    return jnp.dot(selector, rows, preferred_element_type=jnp.float32)


def split_bf16(values):
    upper = values.astype(jnp.bfloat16)
    lower = (values - upper.astype(jnp.float32)).astype(jnp.bfloat16)
    return upper, lower


def spread_rows(selector, terms):
    upper, lower = split_bf16(terms)
    dims = (((0,), (0,)), ((), ()))
    return lax.dot_general(
        selector, upper, dims, preferred_element_type=jnp.float32
    ) + lax.dot_general(selector, lower, dims, preferred_element_type=jnp.float32)


def _sigmoid(x):
    return 1.0 / (1.0 + jnp.exp(-x))


def _select_t(ids_row, total):
    hit = ids_row == lax.broadcasted_iota(jnp.int32, (total, ids_row.shape[1]), 0)
    return jnp.where(hit, 1.0, 0.0).astype(jnp.bfloat16)


def _mm(a, b):
    return jnp.dot(a, b, preferred_element_type=jnp.float32)


def _pick(sel_t, rows):
    return lax.dot_general(sel_t, rows, (((0,), (0,)), ((), ())),
                           preferred_element_type=jnp.float32)


def _spread(sel_t, terms):
    upper = terms.astype(jnp.bfloat16)
    lower = (terms - upper.astype(jnp.float32)).astype(jnp.bfloat16)
    return _mm(sel_t, upper) + _mm(sel_t, lower)


def _chain_body(groups, own_groups, block, neg_count, scale,
                wrow, crow, scomb, srow, nrow, orow, live,
                words, held, table, word_out, ctx_out, slot_out):
    parts = words.shape[0]
    rows = table.shape[0]
    slots = slot_out.shape[0]
    half = words.shape[1] // 2
    word_out[...] = jnp.zeros(word_out.shape, jnp.float32)
    ctx_out[...] = jnp.zeros(ctx_out.shape, jnp.float32)
    slot_sum = jnp.zeros((slot_out.shape[0], words.shape[1]), jnp.float32)
    for g in range(groups):
        t0 = g * block
        word_t = _select_t(wrow[:, t0:t0 + block], parts)
        ctx_t = _select_t(crow[:, t0:t0 + block], parts)
        w = _pick(word_t, words[...])
        c = _pick(ctx_t, held[...])
        rv = _pick(_select_t(scomb[:, t0:t0 + block], rows), table[...])
        w_re, w_im = w[:, :half], w[:, half:]
        r_re, r_im = rv[:, :half], rv[:, half:]
        q = jnp.concatenate([w_re * r_re - w_im * r_im, w_re * r_im + w_im * r_re], axis=1)
        q = q.astype(jnp.bfloat16)
        qf = q.astype(jnp.float32)
        pos = jnp.sum(qf * c, axis=1, keepdims=True)
        dpos = -1.0 / (1.0 + jnp.exp(pos))
        neg_t = _select_t(nrow[g:g + 1, :], parts)
        neg = _pick(neg_t, held[...]).astype(jnp.bfloat16)
        scores = lax.dot_general(q, neg, (((1,), (1,)), ((), ())),
                                 preferred_element_type=jnp.float32)
        dneg = (_sigmoid(scores) * scale).astype(jnp.bfloat16)
        gq = dpos * c + _mm(dneg, neg)
        g_re, g_im = gq[:, :half], gq[:, half:]
        if g < own_groups:
            rterm = jnp.concatenate([g_re * w_re + g_im * w_im, g_im * w_re - g_re * w_im], axis=1)
            slot_sum = slot_sum + _spread(_select_t(srow[:, t0:t0 + block], slots), rterm)
        wterm = jnp.concatenate([g_re * r_re + g_im * r_im, g_im * r_re - g_re * r_im], axis=1)
        word_out[...] += _spread(word_t, wterm)
        neg_weight = lax.dot_general(neg_t, dneg, (((1,), (1,)), ((), ())),
                                     preferred_element_type=jnp.float32)
        ctx_out[...] += _spread(ctx_t, dpos * qf) + _spread(neg_weight, q)
    if own_groups:
        hit = orow[...] == lax.broadcasted_iota(jnp.int32, (rows, orow.shape[1]), 0)
        live_t = jnp.where(hit, live[...], 0.0).astype(jnp.bfloat16)
        slot_sum = slot_sum + 0.02 * _pick(live_t, table[...])
    kept = slot_out.shape[1] // 2
    slot_out[:, :kept] = slot_sum[:, :kept].astype(slot_out.dtype)
    slot_out[:, kept:] = slot_sum[:, half:half + kept].astype(slot_out.dtype)


def block_chains(word_ids, ctx_ids, slot_ids, own_ids, neg_ids, own_groups, scale, words, held,
                 table, own_rows, live_mask, row_width):
    trips = word_ids.shape[0]
    groups, neg_count = neg_ids.shape
    block = trips // groups
    parts, width = words.shape
    body = functools.partial(_chain_body, groups, own_groups, block, neg_count, scale)
    return pl.pallas_call(
        body,
        out_shape=(
            jax.ShapeDtypeStruct((parts, width), jnp.float32),
            jax.ShapeDtypeStruct((parts, width), jnp.float32),
            jax.ShapeDtypeStruct((own_rows.shape[0], row_width), jnp.float32),
        ),
        compiler_params=pltpu.CompilerParams(vmem_limit_bytes=48 * 1024 * 1024),
    )(
        word_ids.reshape(1, -1),
        ctx_ids.reshape(1, -1),
        slot_ids.reshape(1, -1),
        own_ids.reshape(1, -1),
        neg_ids,
        own_rows.reshape(1, -1),
        live_mask.reshape(1, -1),
        words,
        held,
        table,
    )


def lanes_of(half_width):
    return -(-half_width // 128) * 128


def padded_halves(rows, half_width):
    count = rows.shape[0]
    lanes = lanes_of(half_width)
    return jnp.pad(
        rows.reshape(count, 2, half_width), ((0, 0), (0, 0), (0, lanes - half_width))
    ).reshape(count, 2 * lanes)


def unpadded_halves(rows, half_width):
    count = rows.shape[0]
    return rows.reshape(count, 2, lanes_of(half_width))[:, :, :half_width].reshape(
        count, 2 * half_width
    )


def shards(
    words, contexts, relations, word_index, context_index, rel_slot, neg_index, requests, counts
):
    row_width = words.shape[1]
    half_width = row_width // 2
    part_count = lax.axis_size("blk")
    split_count = lax.axis_size("rel")
    owner_count = part_count * split_count
    slot_count = requests.shape[-1]
    slot_total = owner_count * slot_count
    owned_rows = relations.shape[0]
    part_rows = contexts.shape[0]
    trips = word_index.shape[0]
    block_count = neg_index.shape[0]
    neg_count = neg_index.shape[1]
    block_size = trips // block_count
    neg_scale = float(neg_count) ** (-0.5)
    both = ("blk", "rel")

    wanted = requests[0, 0].reshape(owner_count, slot_count)
    incoming = lax.all_to_all(wanted, both, split_axis=0, concat_axis=0, tiled=True)
    lists = incoming.reshape(part_count, split_count, slot_count)
    served = jnp.stack([jnp.roll(lists, -j, axis=1) for j in range(split_count)], axis=2)
    padded_width = 2 * lanes_of(half_width)
    picked = jnp.einsum(
        "dkr,rf->dkf",
        one_hot(served.reshape(owner_count, split_count * slot_count), owned_rows),
        relations,
        preferred_element_type=jnp.float32,
    ).astype(jnp.bfloat16)
    own_ints = jnp.concatenate([word_index, context_index, rel_slot, neg_index.reshape(-1)])
    picked, contexts, own_ints = lax.optimization_barrier((picked, contexts, own_ints))
    held_rows = passed_along(contexts, "blk", 1)

    bucket_ints = jnp.stack(
        [own_ints] + [passed_along(own_ints, "rel", -j) for j in range(1, split_count)]
    )
    word_ids = bucket_ints[:, :trips].reshape(-1)
    ctx_ids = bucket_ints[:, trips : 2 * trips].reshape(-1)
    slot_ids = bucket_ints[:, 2 * trips : 3 * trips]
    slot_ids = (
        (slot_ids // slot_count) * (split_count * slot_count)
        + (jnp.arange(split_count) * slot_count)[:, None]
        + slot_ids % slot_count
    ).reshape(-1)
    own_slots = jnp.arange(slot_total)
    own_rows = (own_slots // slot_count) * (split_count * slot_count) + own_slots % slot_count
    neg_ids = bucket_ints[:, 3 * trips :].reshape(split_count * block_count, neg_count)

    fetched = lax.all_to_all(picked, both, split_axis=0, concat_axis=0, tiled=True)
    live_mask = (
        (jnp.arange(slot_count)[None, :] < counts[0, 0].reshape(owner_count)[:, None])
        .reshape(-1)
        .astype(jnp.float32)
    )

    group_count = split_count * block_count
    word_table = padded_halves(words, half_width)
    held_table = padded_halves(held_rows, half_width)
    fetched, word_table, held_table = lax.optimization_barrier((fetched, word_table, held_table))
    rel_table = padded_halves(fetched.reshape(split_count * slot_total, row_width), half_width)
    own_word, own_ctx, own_slot = block_chains(
        word_ids[:trips], ctx_ids[:trips], slot_ids[:trips], rel_slot, neg_ids[:block_count],
        block_count, neg_scale, word_table, held_table, rel_table, own_rows, live_mask,
        row_width,
    )
    rest_word, rest_ctx, _ = block_chains(
        word_ids[trips:], ctx_ids[trips:], slot_ids[trips:], rel_slot, neg_ids[block_count:],
        0, neg_scale, word_table, held_table, rel_table, own_rows[:8], live_mask[:8],
        row_width,
    )
    word_sum = unpadded_halves(own_word + rest_word, half_width)
    ctx_sum = unpadded_halves(own_ctx + rest_ctx, half_width)
    returned = lax.all_to_all(
        own_slot.astype(jnp.bfloat16).reshape(owner_count, slot_count, row_width),
        both,
        split_axis=0,
        concat_axis=0,
        tiled=True,
    )
    incoming, returned = lax.optimization_barrier((incoming, returned))
    owner_map = one_hot(incoming.reshape(owner_count, slot_count), owned_rows)
    relation_grad = jnp.einsum(
        "dkr,dkf->rf", owner_map, returned, preferred_element_type=jnp.float32
    )
    return (word_sum.astype(jnp.bfloat16), ctx_sum.astype(jnp.bfloat16), relation_grad)


def solution(mesh):
    return jax.shard_map(
        shards,
        mesh=mesh,
        in_specs=(
            P("blk", None),
            P("blk", None),
            P(("blk", "rel"), None),
            P(("blk", "rel")),
            P(("blk", "rel")),
            P(("blk", "rel")),
            P(("blk", "rel"), None),
            P("blk", "rel", None, None, None),
            P("blk", "rel", None, None),
        ),
        out_specs=(P("blk", None), P("blk", None), P(("blk", "rel"), None)),
        check_vma=False,
    )
```
